128 devices in a mesh: prow: 16 (over y, x), pcol: 8 (over z, core).
Axes of the slice: x: 4, y: 4, z: 4, core: 2. Of those that a mesh axis runs over, the one named last changes fastest.
Arguments:
- right_sides: float32 [24, 3, 4, 128, 1024], P(None, None, None, 'prow', 'pcol'), may hold values from -6 to 6
- modulus: float32 [4, 128, 1024], P(None, 'prow', 'pcol'), may hold values from 0.2 to 5
- margin_sides: int32 [16, 8, 4], P('prow', 'pcol'), may hold values 0 or 1
- coarse_vectors: float32 [64, 3, 4, 128, 1024], P(None, None, None, 'prow', 'pcol'), may hold values from -0.013671875 to 0.013671875
- coarse_inverse: float32 [8, 64, 64], P('pcol'), may hold values from -4.256688 to 39.729089
Outputs:
- preconditioned: float32 [24, 3, 4, 128, 1024], P(None, None, None, 'prow', 'pcol')
The draws below stay inside these ranges and needn't reach their ends.
All inputs are finite; a program needn't handle non-finite values. No bound on the sum of `margin_sides` on one device may be relied on, other than what follows from the above.
Results may differ from the reference program's by a relative error of at most 0.00005.
Values sent between devices are 32-bit elements; how exact they have to be, the bound alone decides.
No kernel may reach another device: no remote copies, remote signals or barrier semaphores. Data moves between devices by JAX's collectives and lax.ppermute only.
A program may use at most 128 MiB of HBM per device.

```python
import math
import jax
import jax.numpy as jnp
from jax import lax

CX = 8
CY = 128
PLANES = 4
LOADS = 24
COARSE = 64
NX = 128
NY = 1024
SUBROWS = 16
COLUMNS = 8


def draw_coarse_inverse(key, part):
    magnitude = 0.04 * float(3 * PLANES * NX * CY) ** 0.5
    diagonal_key, coupling_key = jax.random.split(key)
    diagonal = jax.random.uniform(diagonal_key, (COLUMNS, COARSE), jnp.float32, 1.0, 2.0)
    coupling = 0.08 * jnp.clip(jax.random.normal(coupling_key, (COLUMNS, COARSE, COARSE), jnp.float32), -3.0, 3.0)
    coupling = 0.5 * (coupling + jnp.swapaxes(coupling, 1, 2))
    identity = jnp.eye(COARSE, dtype=jnp.float32)
    return magnitude * (coupling + diagonal[:, :, None] * identity[None, :, :])


def with_ends(drawn, key, least, high):
    shape = drawn.shape
    place = [jax.random.randint(jax.random.fold_in(key, axis), (), 0, shape[axis]) for axis in range(len(shape))]
    drawn = drawn.at[tuple(place)].set(least)
    longest = shape.index(max(shape))
    place[longest] = (place[longest] + 1) % shape[longest]
    return drawn.at[tuple(place)].set(high)


def shard_levels(rng, dims, cuts, smallest, high):
    def one(axis_at, parts):
        draws = jax.random.uniform(jax.random.fold_in(jax.random.fold_in(rng, 6), axis_at), (parts,), jnp.float32, smallest / len(cuts), high / len(cuts))
        return jnp.repeat(jnp.exp(draws), dims[axis_at] // parts).reshape((-1,) + (1,) * (len(dims) - axis_at - 1))

    level = one(*cuts[0])
    for cut in cuts[1:]:
        level = level * one(*cut)
    return level


def noise(stream_key, extent, deviation, most, cuts=(), held_as=jnp.bfloat16):
    entries = deviation * jax.random.normal(stream_key, extent, jnp.float32)
    if cuts:
        entries = entries * shard_levels(stream_key, extent, cuts, -0.22, 0.18)
    return jnp.clip(entries, -most, most).astype(held_as)


def setup_inputs(seed: int = 0) -> dict:
    streams_of = jax.random.split(jax.random.key(seed), 6)
    right_sides = noise(streams_of[0], (LOADS, 3, PLANES, NX, NY), 1.0, 6.0, ((3, 16), (4, 8)), jnp.float32)
    modulus = jnp.clip(jnp.exp(math.log(5.0) - 3.218876 * jax.random.uniform(streams_of[1], (PLANES, NX, NY), jnp.float32) ** shard_levels(streams_of[1], (PLANES, NX, NY), ((1, 16), (2, 8)), -0.2, 0.2)), 0.2, 5.0)
    margin_sides = with_ends((jax.random.randint(streams_of[2], (SUBROWS, COLUMNS, 4), 0, 4) < 3).astype(jnp.int32), jax.random.fold_in(streams_of[2], 1), 0, 1)
    coarse_vectors = noise(streams_of[3], (COARSE, 3, PLANES, NX, NY), (3 * PLANES * NX * CY) ** -0.5, 0.013671875, ((3, 16), (4, 8)), jnp.float32)
    coarse_inverse = draw_coarse_inverse(jax.random.fold_in(streams_of[5], 71), 0)
    return dict(right_sides=right_sides, modulus=modulus, margin_sides=margin_sides, coarse_vectors=coarse_vectors, coarse_inverse=coarse_inverse)


RELAX_WEIGHT = 0.7
MASS_SHIFT = 0.5
DIAGONAL_SLOPE = 0.6 + 0.4 / 3.0
BOND_TOTAL = 44.0 / 3.0


def bond_sum(field_padded, modulus_padded, factor_rows, factor_columns):
    plane_count = modulus_padded.shape[0] - 2
    row_count = modulus_padded.shape[1] - 2
    column_count = modulus_padded.shape[2] - 2
    own_field = field_padded[..., 1:-1, 1:-1, 1:-1]
    own_modulus = modulus_padded[1:-1, 1:-1, 1:-1]
    accumulated = MASS_SHIFT * own_field
    for step_p in (-1, 0, 1):
        for step_x in (-1, 0, 1):
            for step_y in (-1, 0, 1):
                if step_p == 0 and step_x == 0 and step_y == 0:
                    continue
                length = step_p * step_p + step_x * step_x + step_y * step_y
                weight = 1.0 / (length * BOND_TOTAL)
                near_field = field_padded[..., 1 + step_p:1 + step_p + plane_count, 1 + step_x:1 + step_x + row_count, 1 + step_y:1 + step_y + column_count]
                near_modulus = modulus_padded[1 + step_p:1 + step_p + plane_count, 1 + step_x:1 + step_x + row_count, 1 + step_y:1 + step_y + column_count]
                factor = factor_rows[step_x + 1] * factor_columns[step_y + 1]
                difference = own_field - factor * near_field
                bond_weight = (0.5 * weight) * (own_modulus + near_modulus)
                direction = (step_p, step_x, step_y)
                projected = 0.0
                for component in range(3):
                    if direction[component] != 0:
                        projected = projected + direction[component] * difference[..., component, :, :, :]
                pieces = []
                for component in range(3):
                    piece = 0.6 * difference[..., component, :, :, :]
                    if direction[component] != 0:
                        piece = piece + (0.4 * direction[component] / length) * projected
                    pieces.append(piece)
                accumulated = accumulated + bond_weight * jnp.stack(pieces, axis=-4)
    return accumulated


def reference(right_sides, modulus, margin_sides, coarse_vectors, coarse_inverse):
    row_index = lax.broadcasted_iota(jnp.int32, (NX, NY), 0)
    column_index = lax.broadcasted_iota(jnp.int32, (NX, NY), 1)
    cell_sides = margin_sides[row_index // CX, column_index // CY].astype(jnp.float32)
    row_place = row_index % CX
    column_place = column_index % CY
    unity = jnp.ones((NX, NY), jnp.float32)
    factor_rows = jnp.stack([jnp.where(row_place == 0, cell_sides[:, :, 0], unity), unity, jnp.where(row_place == CX - 1, cell_sides[:, :, 1], unity)])
    factor_columns = jnp.stack([jnp.where(column_place == 0, cell_sides[:, :, 2], unity), unity, jnp.where(column_place == CY - 1, cell_sides[:, :, 3], unity)])
    diagonal = MASS_SHIFT + DIAGONAL_SLOPE * modulus
    modulus_padded = jnp.pad(modulus, 1)

    def smooth_one(load):
        first = RELAX_WEIGHT * load / diagonal
        first_padded = jnp.pad(first, ((0, 0), (1, 1), (1, 1), (1, 1)))
        applied = bond_sum(first_padded, modulus_padded, factor_rows, factor_columns)
        return first + RELAX_WEIGHT * (load - applied) / diagonal

    smoothed = lax.map(smooth_one, right_sides)
    vectors = coarse_vectors.reshape(COARSE, 3, PLANES, NX, COLUMNS, CY)
    loads = right_sides.reshape(LOADS, 3, PLANES, NX, COLUMNS, CY)
    restricted = jnp.einsum('vcpxjy,kcpxjy->jvk', vectors, loads, precision=lax.Precision.HIGHEST)
    solved = jnp.einsum('jvw,jwk->jvk', coarse_inverse, restricted, precision=lax.Precision.HIGHEST)
    lifted = jnp.einsum('jvk,vcpxjy->kcpxjy', solved, vectors, precision=lax.Precision.HIGHEST)
    return smoothed + lifted.reshape(LOADS, 3, PLANES, NX, NY)
```

```python
import jax
import jax.numpy as jnp
from jax import lax
from jax.sharding import PartitionSpec as P

RELAX_WEIGHT = 0.7
MASS_SHIFT = 0.5
DIAGONAL_SLOPE = 0.6 + 0.4 / 3.0
BOND_TOTAL = 44.0 / 3.0


def extended(x, sides, width):
    for axis, dim in sides:
        size, length = (lax.axis_size(axis), x.shape[dim])
        up = [(i, (i + 1) % size) for i in range(size - 1)]
        down = [(j, i) for i, j in up]
        last = lax.slice_in_dim(x, length - width, length, axis=dim)
        first = lax.slice_in_dim(x, 0, width, axis=dim)
        before = lax.ppermute(last, axis, up)
        after = lax.ppermute(first, axis, down)
        x = jnp.concatenate([before, x, after], axis=dim)
    return x


def butterfly_sum(x, axis):
    size = lax.axis_size(axis)
    step = 1
    while step < size:
        pairs = [(i, i ^ step) for i in range(size)]
        x = x + lax.ppermute(x, axis, pairs)
        step *= 2
    return x


def bond_sum(field_padded, modulus_padded, factor_rows, factor_columns):
    plane_count = modulus_padded.shape[0] - 2
    row_count = modulus_padded.shape[1] - 2
    column_count = modulus_padded.shape[2] - 2
    own_field = field_padded[..., 1:-1, 1:-1, 1:-1]
    own_modulus = modulus_padded[1:-1, 1:-1, 1:-1]
    accumulated = MASS_SHIFT * own_field
    for step_p in (-1, 0, 1):
        for step_x in (-1, 0, 1):
            for step_y in (-1, 0, 1):
                if step_p == 0 and step_x == 0 and (step_y == 0):
                    continue
                length = step_p * step_p + step_x * step_x + step_y * step_y
                weight = 1.0 / (length * BOND_TOTAL)
                near_field = field_padded[
                    ...,
                    1 + step_p : 1 + step_p + plane_count,
                    1 + step_x : 1 + step_x + row_count,
                    1 + step_y : 1 + step_y + column_count,
                ]
                near_modulus = modulus_padded[
                    1 + step_p : 1 + step_p + plane_count,
                    1 + step_x : 1 + step_x + row_count,
                    1 + step_y : 1 + step_y + column_count,
                ]
                factor = factor_rows[step_x + 1] * factor_columns[step_y + 1]
                difference = own_field - factor * near_field
                bond_weight = 0.5 * weight * (own_modulus + near_modulus)
                direction = (step_p, step_x, step_y)
                projected = 0.0
                for component in range(3):
                    if direction[component] != 0:
                        projected = (
                            projected + direction[component] * difference[..., component, :, :, :]
                        )
                pieces = []
                for component in range(3):
                    piece = 0.6 * difference[..., component, :, :, :]
                    if direction[component] != 0:
                        piece = piece + 0.4 * direction[component] / length * projected
                    pieces.append(piece)
                accumulated = accumulated + bond_weight * jnp.stack(pieces, axis=-4)
    return accumulated


def per_device(right_sides, modulus, margin_sides, coarse_vectors, coarse_inverse):
    load_count = right_sides.shape[0]
    plane_count = right_sides.shape[2]
    row_count = right_sides.shape[3]
    column_count = right_sides.shape[4]
    stacked = jnp.concatenate(
        [right_sides.reshape(load_count * 3, plane_count, row_count, column_count), modulus[None]],
        axis=0,
    )
    padded_all = extended(stacked, (("prow", 2), ("pcol", 3)), 1)
    load_halo = padded_all[: load_count * 3].reshape(
        load_count, 3, plane_count, row_count + 2, column_count + 2
    )
    modulus_halo = padded_all[load_count * 3]
    first_halo = RELAX_WEIGHT * load_halo / (MASS_SHIFT + DIAGONAL_SLOPE * modulus_halo)
    first_padded = jnp.pad(first_halo, ((0, 0), (0, 0), (1, 1), (0, 0), (0, 0)))
    modulus_padded = jnp.pad(modulus_halo, ((1, 1), (0, 0), (0, 0)))
    side_values = margin_sides[0, 0].astype(jnp.float32)
    row_index = lax.broadcasted_iota(jnp.int32, (row_count, column_count), 0)
    column_index = lax.broadcasted_iota(jnp.int32, (row_count, column_count), 1)
    unity = jnp.ones((row_count, column_count), jnp.float32)
    factor_rows = jnp.stack(
        [
            jnp.where(row_index == 0, side_values[0], unity),
            unity,
            jnp.where(row_index == row_count - 1, side_values[1], unity),
        ]
    )
    factor_columns = jnp.stack(
        [
            jnp.where(column_index == 0, side_values[2], unity),
            unity,
            jnp.where(column_index == column_count - 1, side_values[3], unity),
        ]
    )
    diagonal = MASS_SHIFT + DIAGONAL_SLOPE * modulus
    first = first_halo[..., 1:-1, 1:-1]
    applied = bond_sum(first_padded, modulus_padded, factor_rows, factor_columns)
    smoothed = first + RELAX_WEIGHT * (right_sides - applied) / diagonal
    flat_vectors = coarse_vectors.reshape(coarse_vectors.shape[0], -1)
    flat_loads = right_sides.reshape(load_count, -1)
    partial_terms = lax.dot_general(
        flat_vectors, flat_loads, (((1,), (1,)), ((), ())), precision=lax.Precision.HIGHEST
    )
    restricted = butterfly_sum(partial_terms, "prow")
    solved = jnp.dot(coarse_inverse[0], restricted, precision=lax.Precision.HIGHEST)
    lifted = lax.dot_general(
        solved, flat_vectors, (((0,), (0,)), ((), ())), precision=lax.Precision.HIGHEST
    )
    return smoothed + lifted.reshape(right_sides.shape)


def solution(mesh):
    in_specs = (
        P(None, None, None, "prow", "pcol"),
        P(None, "prow", "pcol"),
        P("prow", "pcol", None),
        P(None, None, None, "prow", "pcol"),
        P("pcol", None, None),
    )
    out_specs = P(None, None, None, "prow", "pcol")
    return jax.shard_map(
        per_device, mesh=mesh, in_specs=in_specs, out_specs=out_specs, check_vma=False
    )
```

```python
import jax
import jax.numpy as jnp
from jax import lax
from jax.experimental import pallas as pl
from jax.experimental.pallas import tpu as pltpu
from jax.sharding import PartitionSpec as P

RELAX_WEIGHT = 0.7
MASS_SHIFT = 0.5
DIAGONAL_SLOPE = 0.6 + 0.4 / 3.0
BOND_TOTAL = 44.0 / 3.0

OFFSETS = [
    (step_p, step_x, step_y)
    for step_p in (-1, 0, 1)
    for step_x in (-1, 0, 1)
    for step_y in (-1, 0, 1)
    if (step_p, step_x, step_y) != (0, 0, 0)
]
OWN_ENTRIES = ((0, 0), (1, 1), (2, 2), (0, 1), (0, 2), (1, 2))


def butterfly_sum(x, axis):
    size = lax.axis_size(axis)
    step = 1
    while step < size:
        pairs = [(i, i ^ step) for i in range(size)]
        x = x + lax.ppermute(x, axis, pairs)
        step *= 2
    return x


def neighbour_shift(tile, row_lo, row_hi, col_lo, col_hi, step_x, step_y):
    rows, cols = tile.shape
    if step_x != 0:
        rolled = pltpu.roll(tile, (-step_x) % rows, 0)
        sub = lax.broadcasted_iota(jnp.int32, tile.shape, 0)
        edge = rows - 1 if step_x > 0 else 0
        halo = row_hi if step_x > 0 else row_lo
        tile = jnp.where(sub == edge, jnp.broadcast_to(halo, tile.shape), rolled)
    if step_y != 0:
        rolled = pltpu.roll(tile, (-step_y) % cols, 1)
        lane = lax.broadcasted_iota(jnp.int32, tile.shape, 1)
        edge = cols - 1 if step_y > 0 else 0
        halo = col_hi if step_y > 0 else col_lo
        tile = jnp.where(lane == edge, jnp.broadcast_to(halo, tile.shape), rolled)
    return tile


def smoother_kernel(
    sides_ref, rs_ref, mod_ref, rlo_ref, rhi_ref, clo_ref, chi_ref, out_ref, coef_ref, own_ref, inv_ref,
    frlo_ref, frhi_ref, fclo_ref, fchi_ref,
):
    channels, planes, rows, cols = rs_ref.shape
    loads = channels // 3
    mod_channel = channels
    shape = (rows, cols)
    sub = lax.broadcasted_iota(jnp.int32, shape, 0)
    lane = lax.broadcasted_iota(jnp.int32, shape, 1)
    one = jnp.ones(shape, jnp.float32)
    factor_x = {
        -1: jnp.where(sub == 0, sides_ref[0], one),
        0: None,
        1: jnp.where(sub == rows - 1, sides_ref[1], one),
    }
    factor_y = {
        -1: jnp.where(lane == 0, sides_ref[2], one),
        0: None,
        1: jnp.where(lane == cols - 1, sides_ref[3], one),
    }

    def halo_pieces(refs, channel, plane, step_x):
        row_lo = refs[0][channel, pl.ds(plane, 1), :]
        row_hi = refs[1][channel, pl.ds(plane, 1), :]
        col_lo = refs[2][channel, plane, pl.ds(1 + step_x, rows), :]
        col_hi = refs[3][channel, plane, pl.ds(1 + step_x, rows), :]
        return row_lo, row_hi, col_lo, col_hi

    raw_halos = (rlo_ref, rhi_ref, clo_ref, chi_ref)
    first_halos = (frlo_ref, frhi_ref, fclo_ref, fchi_ref)
    for raw, first in zip(raw_halos, first_halos):
        first[...] = RELAX_WEIGHT * raw[0:channels] / (
            MASS_SHIFT + DIAGONAL_SLOPE * raw[mod_channel : mod_channel + 1]
        )

    for plane in range(planes):
        own_modulus = mod_ref[plane]
        inv_ref[plane] = 1.0 / (MASS_SHIFT + DIAGONAL_SLOPE * own_modulus)
        own = [None] * 6
        for index, (step_p, step_x, step_y) in enumerate(OFFSETS):
            source = plane + step_p
            length = step_p * step_p + step_x * step_x + step_y * step_y
            weight = 1.0 / (length * BOND_TOTAL)
            if 0 <= source < planes:
                pieces = halo_pieces(raw_halos, mod_channel, source, step_x)
                near_modulus = neighbour_shift(mod_ref[source], *pieces, step_x, step_y)
                bond = (0.5 * weight) * (own_modulus + near_modulus)
                coefficient = bond
                if factor_x[step_x] is not None:
                    coefficient = coefficient * factor_x[step_x]
                if factor_y[step_y] is not None:
                    coefficient = coefficient * factor_y[step_y]
                coef_ref[0, index, plane] = 0.6 * coefficient
                coef_ref[1, index, plane] = (0.4 / length) * coefficient
            else:
                bond = (0.5 * weight) * own_modulus
            direction = (step_p, step_x, step_y)
            for entry, (a, b) in enumerate(OWN_ENTRIES):
                scale = 0.4 * direction[a] * direction[b] / length
                if a == b:
                    scale += 0.6
                if scale == 0.0:
                    continue
                term = scale * bond
                own[entry] = term if own[entry] is None else own[entry] + term
        for entry, (a, b) in enumerate(OWN_ENTRIES):
            value = own[entry]
            if a == b:
                value = value + MASS_SHIFT
            own_ref[entry, plane] = value

    def one_load(load, carry):
        base = load * 3
        first = [[None] * planes for _ in range(3)]
        for component in range(3):
            for plane in range(planes):
                first[component][plane] = (
                    RELAX_WEIGHT * rs_ref[base + component, plane] * inv_ref[plane]
                )
        applied = [[None] * 3 for _ in range(planes)]
        for plane in range(planes):
            f = [first[k][plane] for k in range(3)]
            own = [own_ref[e, plane] for e in range(6)]
            applied[plane][0] = own[0] * f[0] + own[3] * f[1] + own[4] * f[2]
            applied[plane][1] = own[3] * f[0] + own[1] * f[1] + own[5] * f[2]
            applied[plane][2] = own[4] * f[0] + own[5] * f[1] + own[2] * f[2]
        for source in range(planes):
            for step_x in (-1, 0, 1):
                for step_y in (-1, 0, 1):
                    targets = [
                        (source - step_p, step_p)
                        for step_p in (-1, 0, 1)
                        if 0 <= source - step_p < planes and (step_p, step_x, step_y) != (0, 0, 0)
                    ]
                    if not targets:
                        continue
                    near = []
                    for component in range(3):
                        pieces = halo_pieces(first_halos, base + component, source, step_x)
                        near.append(
                            neighbour_shift(first[component][source], *pieces, step_x, step_y)
                        )
                    for plane, step_p in targets:
                        direction = (step_p, step_x, step_y)
                        index = OFFSETS.index(direction)
                        projected = None
                        for component in range(3):
                            if direction[component] == 0:
                                continue
                            term = near[component]
                            if projected is None:
                                projected = term if direction[component] > 0 else -term
                            elif direction[component] > 0:
                                projected = projected + term
                            else:
                                projected = projected - term
                        along = coef_ref[1, index, plane] * projected
                        straight = coef_ref[0, index, plane]
                        for component in range(3):
                            value = applied[plane][component] - straight * near[component]
                            if direction[component] > 0:
                                value = value - along
                            elif direction[component] < 0:
                                value = value + along
                            applied[plane][component] = value
        for component in range(3):
            for plane in range(planes):
                load_tile = rs_ref[base + component, plane]
                out_ref[base + component, plane] = first[component][plane] + RELAX_WEIGHT * (
                    load_tile - applied[plane][component]
                ) * inv_ref[plane]
        return carry

    lax.fori_loop(0, loads, one_load, 0)


def smoother(sides, loads, modulus, row_lo, row_hi, col_lo, col_hi):
    channels, planes, rows, cols = loads.shape
    vmem = pltpu.MemorySpace.VMEM
    return pl.pallas_call(
        smoother_kernel,
        out_shape=jax.ShapeDtypeStruct(loads.shape, jnp.float32),
        in_specs=[pl.BlockSpec(memory_space=pltpu.MemorySpace.SMEM)]
        + [pl.BlockSpec(memory_space=vmem)] * 6,
        out_specs=pl.BlockSpec(memory_space=vmem),
        scratch_shapes=[
            pltpu.VMEM((2, len(OFFSETS), planes, rows, cols), jnp.float32),
            pltpu.VMEM((6, planes, rows, cols), jnp.float32),
            pltpu.VMEM((planes, rows, cols), jnp.float32),
            pltpu.VMEM((channels,) + row_lo.shape[1:], jnp.float32),
            pltpu.VMEM((channels,) + row_hi.shape[1:], jnp.float32),
            pltpu.VMEM((channels,) + col_lo.shape[1:], jnp.float32),
            pltpu.VMEM((channels,) + col_hi.shape[1:], jnp.float32),
        ],
    )(sides, loads, modulus, row_lo, row_hi, col_lo, col_hi)


def per_device(right_sides, modulus, margin_sides, coarse_vectors, coarse_inverse):
    load_count = right_sides.shape[0]
    plane_count = right_sides.shape[2]
    row_count = right_sides.shape[3]
    column_count = right_sides.shape[4]
    flat_vectors = coarse_vectors.reshape(coarse_vectors.shape[0], -1)
    flat_loads = right_sides.reshape(load_count, -1)
    partial_terms = lax.dot_general(
        flat_vectors, flat_loads, (((1,), (1,)), ((), ())), precision=lax.Precision.HIGHEST
    )
    restricted = butterfly_sum(partial_terms, "prow")

    loads = right_sides.reshape(load_count * 3, plane_count, row_count, column_count)
    stacked = jnp.concatenate([loads, modulus[None]], axis=0)
    prow_size = lax.axis_size("prow")
    up = [(i, i + 1) for i in range(prow_size - 1)]
    down = [(i + 1, i) for i in range(prow_size - 1)]
    row_lo = lax.ppermute(stacked[:, :, row_count - 1, :], "prow", up)
    row_hi = lax.ppermute(stacked[:, :, 0, :], "prow", down)
    pcol_size = lax.axis_size("pcol")
    up = [(i, i + 1) for i in range(pcol_size - 1)]
    down = [(i + 1, i) for i in range(pcol_size - 1)]
    last_column = jnp.concatenate(
        [row_lo[:, :, None, column_count - 1], stacked[:, :, :, column_count - 1], row_hi[:, :, None, column_count - 1]],
        axis=2,
    )
    first_column = jnp.concatenate(
        [row_lo[:, :, None, 0], stacked[:, :, :, 0], row_hi[:, :, None, 0]], axis=2
    )
    col_lo = lax.ppermute(last_column, "pcol", up)[..., None]
    col_hi = lax.ppermute(first_column, "pcol", down)[..., None]
    sides = margin_sides[0, 0].astype(jnp.float32)
    smoothed = smoother(sides, loads, modulus, row_lo, row_hi, col_lo, col_hi)

    solved = jnp.dot(coarse_inverse[0], restricted, precision=lax.Precision.HIGHEST)
    lifted = lax.dot_general(
        solved, flat_vectors, (((0,), (0,)), ((), ())), precision=lax.Precision.HIGHEST
    )
    return smoothed.reshape(right_sides.shape) + lifted.reshape(right_sides.shape)


def solution(mesh):
    in_specs = (
        P(None, None, None, "prow", "pcol"),
        P(None, "prow", "pcol"),
        P("prow", "pcol", None),
        P(None, None, None, "prow", "pcol"),
        P("pcol", None, None),
    )
    out_specs = P(None, None, None, "prow", "pcol")
    return jax.shard_map(
        per_device, mesh=mesh, in_specs=in_specs, out_specs=out_specs, check_vma=False
    )
```

```python
import jax
import jax.numpy as jnp
from jax import lax
from jax.experimental import pallas as pl
from jax.experimental.pallas import tpu as pltpu
from jax.sharding import PartitionSpec as P

RELAX_WEIGHT = 0.7
MASS_SHIFT = 0.5
DIAGONAL_SLOPE = 0.6 + 0.4 / 3.0
BOND_TOTAL = 44.0 / 3.0

OFFSETS = [
    (step_p, step_x, step_y)
    for step_p in (-1, 0, 1)
    for step_x in (-1, 0, 1)
    for step_y in (-1, 0, 1)
    if (step_p, step_x, step_y) != (0, 0, 0)
]
OWN_ENTRIES = ((0, 0), (1, 1), (2, 2), (0, 1), (0, 2), (1, 2))


def butterfly_sum(x, axis):
    size = lax.axis_size(axis)
    step = 1
    while step < size:
        pairs = [(i, i ^ step) for i in range(size)]
        x = x + lax.ppermute(x, axis, pairs)
        step *= 2
    return x


def neighbour_shift(tile, row_lo, row_hi, col_lo, col_hi, step_x, step_y):
    rows, cols = tile.shape
    if step_x != 0:
        rolled = pltpu.roll(tile, (-step_x) % rows, 0)
        sub = lax.broadcasted_iota(jnp.int32, tile.shape, 0)
        edge = rows - 1 if step_x > 0 else 0
        halo = row_hi if step_x > 0 else row_lo
        tile = jnp.where(sub == edge, jnp.broadcast_to(halo, tile.shape), rolled)
    if step_y != 0:
        rolled = pltpu.roll(tile, (-step_y) % cols, 1)
        lane = lax.broadcasted_iota(jnp.int32, tile.shape, 1)
        edge = cols - 1 if step_y > 0 else 0
        halo = col_hi if step_y > 0 else col_lo
        tile = jnp.where(lane == edge, jnp.broadcast_to(halo, tile.shape), rolled)
    return tile


def pack_kernel(rs_ref, mod_ref, row_first_ref, row_last_ref, col_first_ref, col_last_ref):
    channels, planes, rows, cols = rs_ref.shape
    lane = lax.broadcasted_iota(jnp.int32, (rows, cols), 1)
    tiles = col_first_ref.shape[1] // cols
    first = [jnp.zeros((rows, cols), jnp.float32) for _ in range(tiles)]
    last = [jnp.zeros((rows, cols), jnp.float32) for _ in range(tiles)]
    for channel in range(channels + 1):
        for plane in range(planes):
            tile = rs_ref[channel, plane] if channel < channels else mod_ref[plane]
            j = channel * planes + plane
            row_first_ref[pl.ds(j, 1), :] = tile[0:1, :]
            row_last_ref[pl.ds(j, 1), :] = tile[rows - 1 : rows, :]
            group, place = divmod(j, cols)
            first[group] = jnp.where(lane == place, pltpu.roll(tile, place, 1), first[group])
            last[group] = jnp.where(
                lane == place, pltpu.roll(tile, (place + 1) % cols, 1), last[group]
            )
    for group in range(tiles):
        col_first_ref[:, pl.ds(group * cols, cols)] = first[group]
        col_last_ref[:, pl.ds(group * cols, cols)] = last[group]


def pack(loads, modulus):
    channels, planes, rows, cols = loads.shape
    count = (channels + 1) * planes
    lanes = -(-count // cols) * cols
    vmem = pltpu.MemorySpace.VMEM
    return pl.pallas_call(
        pack_kernel,
        out_shape=[
            jax.ShapeDtypeStruct((count, cols), jnp.float32),
            jax.ShapeDtypeStruct((count, cols), jnp.float32),
            jax.ShapeDtypeStruct((rows, lanes), jnp.float32),
            jax.ShapeDtypeStruct((rows, lanes), jnp.float32),
        ],
        in_specs=[pl.BlockSpec(memory_space=vmem)] * 2,
        out_specs=[pl.BlockSpec(memory_space=vmem)] * 4,
    )(loads, modulus)


def smoother_kernel(
    sides_ref, rs_ref, mod_ref, rlo_ref, rhi_ref, clo_ref, chi_ref,
    cll_ref, clh_ref, chl_ref, chh_ref,
    out_ref, coef_ref, own_ref, inv_ref, row_ref, col_ref,
):
    channels, planes, rows, cols = rs_ref.shape
    loads = channels // 3
    mod_channel = channels
    shape = (rows, cols)
    sub = lax.broadcasted_iota(jnp.int32, shape, 0)
    lane = lax.broadcasted_iota(jnp.int32, shape, 1)
    one = jnp.ones(shape, jnp.float32)
    factor_x = {
        -1: jnp.where(sub == 0, sides_ref[0], one),
        0: None,
        1: jnp.where(sub == rows - 1, sides_ref[1], one),
    }
    factor_y = {
        -1: jnp.where(lane == 0, sides_ref[2], one),
        0: None,
        1: jnp.where(lane == cols - 1, sides_ref[3], one),
    }

    def halo_pieces(channel, plane, step_x):
        row_lo = row_ref[0, channel, pl.ds(plane, 1), :]
        row_hi = row_ref[1, channel, pl.ds(plane, 1), :]
        col_lo = col_ref[0, channel, plane, pl.ds(1 + step_x, rows), :]
        col_hi = col_ref[1, channel, plane, pl.ds(1 + step_x, rows), :]
        return row_lo, row_hi, col_lo, col_hi

    for channel in range(channels + 1):
        row_ref[0, channel] = rlo_ref[pl.ds(channel * planes, planes), :]
        row_ref[1, channel] = rhi_ref[pl.ds(channel * planes, planes), :]
        for plane in range(planes):
            j = channel * planes + plane
            group, place = divmod(j, cols)
            window = pl.ds(group * cols, cols)
            for side, (edge, column, corner_lo, corner_hi) in enumerate(
                ((0, clo_ref, cll_ref, chl_ref), (cols - 1, chi_ref, clh_ref, chh_ref))
            ):
                shift = (edge - place) % cols
                col_ref[side, channel, plane, pl.ds(1, rows), :] = pltpu.roll(
                    column[:, window], shift, 1
                )
                col_ref[side, channel, plane, pl.ds(0, 1), :] = pltpu.roll(
                    corner_lo[pl.ds(rows - 1, 1), window], shift, 1
                )
                col_ref[side, channel, plane, pl.ds(rows + 1, 1), :] = pltpu.roll(
                    corner_hi[pl.ds(0, 1), window], shift, 1
                )
    row_inverse = RELAX_WEIGHT / (MASS_SHIFT + DIAGONAL_SLOPE * row_ref[:, mod_channel : mod_channel + 1])
    row_ref[:, 0:channels] = row_ref[:, 0:channels] * row_inverse
    col_inverse = RELAX_WEIGHT / (MASS_SHIFT + DIAGONAL_SLOPE * col_ref[:, mod_channel : mod_channel + 1, :, 0 : rows + 2])
    col_ref[:, 0:channels, :, 0 : rows + 2] = col_ref[:, 0:channels, :, 0 : rows + 2] * col_inverse

    for plane in range(planes):
        own_modulus = mod_ref[plane]
        inv_ref[plane] = 1.0 / (MASS_SHIFT + DIAGONAL_SLOPE * own_modulus)
        own = [None] * 6
        for index, (step_p, step_x, step_y) in enumerate(OFFSETS):
            source = plane + step_p
            length = step_p * step_p + step_x * step_x + step_y * step_y
            weight = 1.0 / (length * BOND_TOTAL)
            if 0 <= source < planes:
                pieces = halo_pieces(mod_channel, source, step_x)
                near_modulus = neighbour_shift(mod_ref[source], *pieces, step_x, step_y)
                bond = (0.5 * weight) * (own_modulus + near_modulus)
                coefficient = bond
                if factor_x[step_x] is not None:
                    coefficient = coefficient * factor_x[step_x]
                if factor_y[step_y] is not None:
                    coefficient = coefficient * factor_y[step_y]
                coef_ref[0, index, plane] = 0.6 * coefficient
                coef_ref[1, index, plane] = (0.4 / length) * coefficient
            else:
                bond = (0.5 * weight) * own_modulus
            direction = (step_p, step_x, step_y)
            for entry, (a, b) in enumerate(OWN_ENTRIES):
                scale = 0.4 * direction[a] * direction[b] / length
                if a == b:
                    scale += 0.6
                if scale == 0.0:
                    continue
                term = scale * bond
                own[entry] = term if own[entry] is None else own[entry] + term
        for entry, (a, b) in enumerate(OWN_ENTRIES):
            value = own[entry]
            if a == b:
                value = value + MASS_SHIFT
            own_ref[entry, plane] = value

    def one_load(load, carry):
        base = load * 3
        first = [[None] * planes for _ in range(3)]
        for component in range(3):
            for plane in range(planes):
                first[component][plane] = (
                    RELAX_WEIGHT * rs_ref[base + component, plane] * inv_ref[plane]
                )
        applied = [[None] * 3 for _ in range(planes)]
        for plane in range(planes):
            f = [first[k][plane] for k in range(3)]
            own = [own_ref[e, plane] for e in range(6)]
            applied[plane][0] = own[0] * f[0] + own[3] * f[1] + own[4] * f[2]
            applied[plane][1] = own[3] * f[0] + own[1] * f[1] + own[5] * f[2]
            applied[plane][2] = own[4] * f[0] + own[5] * f[1] + own[2] * f[2]
        for source in range(planes):
            for step_x in (-1, 0, 1):
                for step_y in (-1, 0, 1):
                    targets = [
                        (source - step_p, step_p)
                        for step_p in (-1, 0, 1)
                        if 0 <= source - step_p < planes and (step_p, step_x, step_y) != (0, 0, 0)
                    ]
                    if not targets:
                        continue
                    near = []
                    for component in range(3):
                        pieces = halo_pieces(base + component, source, step_x)
                        near.append(
                            neighbour_shift(first[component][source], *pieces, step_x, step_y)
                        )
                    for plane, step_p in targets:
                        direction = (step_p, step_x, step_y)
                        index = OFFSETS.index(direction)
                        projected = None
                        for component in range(3):
                            if direction[component] == 0:
                                continue
                            term = near[component]
                            if projected is None:
                                projected = term if direction[component] > 0 else -term
                            elif direction[component] > 0:
                                projected = projected + term
                            else:
                                projected = projected - term
                        along = coef_ref[1, index, plane] * projected
                        straight = coef_ref[0, index, plane]
                        for component in range(3):
                            value = applied[plane][component] - straight * near[component]
                            if direction[component] > 0:
                                value = value - along
                            elif direction[component] < 0:
                                value = value + along
                            applied[plane][component] = value
        for component in range(3):
            for plane in range(planes):
                load_tile = rs_ref[base + component, plane]
                out_ref[base + component, plane] = first[component][plane] + RELAX_WEIGHT * (
                    load_tile - applied[plane][component]
                ) * inv_ref[plane]
        return carry

    lax.fori_loop(0, loads, one_load, 0)


def smoother(sides, loads, modulus, halos):
    channels, planes, rows, cols = loads.shape
    vmem = pltpu.MemorySpace.VMEM
    return pl.pallas_call(
        smoother_kernel,
        out_shape=jax.ShapeDtypeStruct(loads.shape, jnp.float32),
        in_specs=[pl.BlockSpec(memory_space=pltpu.MemorySpace.SMEM)]
        + [pl.BlockSpec(memory_space=vmem)] * (2 + len(halos)),
        out_specs=pl.BlockSpec(memory_space=vmem),
        scratch_shapes=[
            pltpu.VMEM((2, len(OFFSETS), planes, rows, cols), jnp.float32),
            pltpu.VMEM((6, planes, rows, cols), jnp.float32),
            pltpu.VMEM((planes, rows, cols), jnp.float32),
            pltpu.VMEM((2, channels + 1, planes, cols), jnp.float32),
            pltpu.VMEM((2, channels + 1, planes, 2 * rows, cols), jnp.float32),
        ],
    )(sides, loads, modulus, *halos)


def per_device(right_sides, modulus, margin_sides, coarse_vectors, coarse_inverse):
    load_count = right_sides.shape[0]
    plane_count = right_sides.shape[2]
    row_count = right_sides.shape[3]
    column_count = right_sides.shape[4]
    cell_dims = (1, 2, 3, 4)
    partial_terms = lax.dot_general(
        coarse_vectors, right_sides, ((cell_dims, cell_dims), ((), ())), precision=lax.Precision.HIGHEST
    )
    restricted = butterfly_sum(partial_terms, "prow")

    loads = right_sides.reshape(load_count * 3, plane_count, row_count, column_count)
    row_first, row_last, col_first, col_last = pack(loads, modulus)
    rows_n = lax.axis_size("prow")
    cols_n = lax.axis_size("pcol")

    def line(source, axis, size, step):
        pairs = [(i, i + step) for i in range(size) if 0 <= i + step < size]
        return lax.ppermute(source, axis, pairs)

    def diagonal(source, step_row, step_col):
        pairs = []
        for a in range(rows_n):
            for b in range(cols_n):
                if 0 <= a + step_row < rows_n and 0 <= b + step_col < cols_n:
                    pairs.append((a * cols_n + b, (a + step_row) * cols_n + b + step_col))
        return lax.ppermute(source, ("prow", "pcol"), pairs)

    halos = (
        line(row_last, "prow", rows_n, 1),
        line(row_first, "prow", rows_n, -1),
        line(col_last, "pcol", cols_n, 1),
        line(col_first, "pcol", cols_n, -1),
        diagonal(col_last, 1, 1),
        diagonal(col_first, 1, -1),
        diagonal(col_last, -1, 1),
        diagonal(col_first, -1, -1),
    )
    sides = margin_sides[0, 0].astype(jnp.float32)
    smoothed = smoother(sides, loads, modulus, halos)

    solved = jnp.dot(coarse_inverse[0], restricted, precision=lax.Precision.HIGHEST)
    lifted = lax.dot_general(
        solved, coarse_vectors, (((0,), (0,)), ((), ())), precision=lax.Precision.HIGHEST
    )
    return smoothed.reshape(right_sides.shape) + lifted


def solution(mesh):
    in_specs = (
        P(None, None, None, "prow", "pcol"),
        P(None, "prow", "pcol"),
        P("prow", "pcol", None),
        P(None, None, None, "prow", "pcol"),
        P("pcol", None, None),
    )
    out_specs = P(None, None, None, "prow", "pcol")
    return jax.shard_map(
        per_device, mesh=mesh, in_specs=in_specs, out_specs=out_specs, check_vma=False
    )
```

```python
import jax
import jax.numpy as jnp
from jax import lax
from jax.experimental import pallas as pl
from jax.experimental.pallas import tpu as pltpu
from jax.sharding import PartitionSpec as P

RELAX_WEIGHT = 0.7
MASS_SHIFT = 0.5
DIAGONAL_SLOPE = 0.6 + 0.4 / 3.0
BOND_TOTAL = 44.0 / 3.0

OFFSETS = [
    (step_p, step_x, step_y)
    for step_p in (-1, 0, 1)
    for step_x in (-1, 0, 1)
    for step_y in (-1, 0, 1)
    if (step_p, step_x, step_y) != (0, 0, 0)
]
OWN_ENTRIES = ((0, 0), (1, 1), (2, 2), (0, 1), (0, 2), (1, 2))


def butterfly_sum(x, axis):
    size = lax.axis_size(axis)
    step = 1
    while step < size:
        pairs = [(i, i ^ step) for i in range(size)]
        x = x + lax.ppermute(x, axis, pairs)
        step *= 2
    return x


def neighbour_shift(tile, row_lo, row_hi, col_lo, col_hi, step_x, step_y):
    rows, cols = tile.shape
    if step_x != 0:
        rolled = pltpu.roll(tile, (-step_x) % rows, 0)
        sub = lax.broadcasted_iota(jnp.int32, tile.shape, 0)
        edge = rows - 1 if step_x > 0 else 0
        halo = row_hi if step_x > 0 else row_lo
        tile = jnp.where(sub == edge, jnp.broadcast_to(halo, tile.shape), rolled)
    if step_y != 0:
        rolled = pltpu.roll(tile, (-step_y) % cols, 1)
        lane = lax.broadcasted_iota(jnp.int32, tile.shape, 1)
        edge = cols - 1 if step_y > 0 else 0
        halo = col_hi if step_y > 0 else col_lo
        tile = jnp.where(lane == edge, jnp.broadcast_to(halo, tile.shape), rolled)
    return tile


def pack_kernel(rs_ref, mod_ref, row_first_ref, row_last_ref, col_first_ref, col_last_ref):
    channels, planes, rows, cols = rs_ref.shape
    lane = lax.broadcasted_iota(jnp.int32, (rows, cols), 1)
    tiles = col_first_ref.shape[1] // cols
    first = [jnp.zeros((rows, cols), jnp.float32) for _ in range(tiles)]
    last = [jnp.zeros((rows, cols), jnp.float32) for _ in range(tiles)]
    for channel in range(channels + 1):
        for plane in range(planes):
            tile = rs_ref[channel, plane] if channel < channels else mod_ref[plane]
            j = channel * planes + plane
            row_first_ref[pl.ds(j, 1), :] = tile[0:1, :]
            row_last_ref[pl.ds(j, 1), :] = tile[rows - 1 : rows, :]
            group, place = divmod(j, cols)
            first[group] = jnp.where(lane == place, pltpu.roll(tile, place, 1), first[group])
            last[group] = jnp.where(
                lane == place, pltpu.roll(tile, (place + 1) % cols, 1), last[group]
            )
    for group in range(tiles):
        col_first_ref[:, pl.ds(group * cols, cols)] = first[group]
        col_last_ref[:, pl.ds(group * cols, cols)] = last[group]


def pack(loads, modulus):
    channels, planes, rows, cols = loads.shape
    count = (channels + 1) * planes
    lanes = -(-count // cols) * cols
    vmem = pltpu.MemorySpace.VMEM
    return pl.pallas_call(
        pack_kernel,
        out_shape=[
            jax.ShapeDtypeStruct((count, cols), jnp.float32),
            jax.ShapeDtypeStruct((count, cols), jnp.float32),
            jax.ShapeDtypeStruct((rows, lanes), jnp.float32),
            jax.ShapeDtypeStruct((rows, lanes), jnp.float32),
        ],
        in_specs=[pl.BlockSpec(memory_space=vmem)] * 2,
        out_specs=[pl.BlockSpec(memory_space=vmem)] * 4,
    )(loads, modulus)


def smoother_kernel(
    sides_ref, rs_ref, mod_ref, rlo_ref, rhi_ref, clo_ref, chi_ref,
    cll_ref, clh_ref, chl_ref, chh_ref,
    out_ref, coef_ref, own_ref, inv_ref, row_ref, col_ref,
):
    channels, planes, rows, cols = rs_ref.shape
    loads = channels // 3
    mod_channel = channels
    shape = (rows, cols)
    sub = lax.broadcasted_iota(jnp.int32, shape, 0)
    lane = lax.broadcasted_iota(jnp.int32, shape, 1)
    one = jnp.ones(shape, jnp.float32)
    factor_x = {
        -1: jnp.where(sub == 0, sides_ref[0], one),
        0: None,
        1: jnp.where(sub == rows - 1, sides_ref[1], one),
    }
    factor_y = {
        -1: jnp.where(lane == 0, sides_ref[2], one),
        0: None,
        1: jnp.where(lane == cols - 1, sides_ref[3], one),
    }

    def halo_pieces(channel, plane, step_x):
        row_lo = row_ref[0, channel, pl.ds(plane, 1), :]
        row_hi = row_ref[1, channel, pl.ds(plane, 1), :]
        col_lo = col_ref[0, channel, plane, pl.ds(1 + step_x, rows), :]
        col_hi = col_ref[1, channel, plane, pl.ds(1 + step_x, rows), :]
        return row_lo, row_hi, col_lo, col_hi

    for channel in range(channels + 1):
        row_ref[0, channel] = rlo_ref[pl.ds(channel * planes, planes), :]
        row_ref[1, channel] = rhi_ref[pl.ds(channel * planes, planes), :]
        for plane in range(planes):
            j = channel * planes + plane
            group, place = divmod(j, cols)
            window = pl.ds(group * cols, cols)
            for side, (edge, column, corner_lo, corner_hi) in enumerate(
                ((0, clo_ref, cll_ref, chl_ref), (cols - 1, chi_ref, clh_ref, chh_ref))
            ):
                shift = (edge - place) % cols
                col_ref[side, channel, plane, pl.ds(1, rows), :] = pltpu.roll(
                    column[:, window], shift, 1
                )
                col_ref[side, channel, plane, pl.ds(0, 1), :] = pltpu.roll(
                    corner_lo[pl.ds(rows - 1, 1), window], shift, 1
                )
                col_ref[side, channel, plane, pl.ds(rows + 1, 1), :] = pltpu.roll(
                    corner_hi[pl.ds(0, 1), window], shift, 1
                )
    row_inverse = RELAX_WEIGHT / (MASS_SHIFT + DIAGONAL_SLOPE * row_ref[:, mod_channel : mod_channel + 1])
    row_ref[:, 0:channels] = row_ref[:, 0:channels] * row_inverse
    col_inverse = RELAX_WEIGHT / (MASS_SHIFT + DIAGONAL_SLOPE * col_ref[:, mod_channel : mod_channel + 1, :, 0 : rows + 2])
    col_ref[:, 0:channels, :, 0 : rows + 2] = col_ref[:, 0:channels, :, 0 : rows + 2] * col_inverse

    for plane in range(planes):
        own_modulus = mod_ref[plane]
        inv_ref[plane] = 1.0 / (MASS_SHIFT + DIAGONAL_SLOPE * own_modulus)
        own = [None] * 6
        for index, (step_p, step_x, step_y) in enumerate(OFFSETS):
            source = plane + step_p
            length = step_p * step_p + step_x * step_x + step_y * step_y
            weight = 1.0 / (length * BOND_TOTAL)
            if 0 <= source < planes:
                pieces = halo_pieces(mod_channel, source, step_x)
                near_modulus = neighbour_shift(mod_ref[source], *pieces, step_x, step_y)
                bond = (0.5 * weight) * (own_modulus + near_modulus)
                coefficient = bond
                if factor_x[step_x] is not None:
                    coefficient = coefficient * factor_x[step_x]
                if factor_y[step_y] is not None:
                    coefficient = coefficient * factor_y[step_y]
                coef_ref[0, index, plane] = 0.6 * coefficient
                coef_ref[1, index, plane] = (0.4 / length) * coefficient
            else:
                bond = (0.5 * weight) * own_modulus
            direction = (step_p, step_x, step_y)
            for entry, (a, b) in enumerate(OWN_ENTRIES):
                scale = 0.4 * direction[a] * direction[b] / length
                if a == b:
                    scale += 0.6
                if scale == 0.0:
                    continue
                term = scale * bond
                own[entry] = term if own[entry] is None else own[entry] + term
        for entry, (a, b) in enumerate(OWN_ENTRIES):
            value = own[entry]
            if a == b:
                value = value + MASS_SHIFT
            own_ref[entry, plane] = value

    def one_load(load, carry):
        base = load * 3
        first = [[None] * planes for _ in range(3)]
        for component in range(3):
            for plane in range(planes):
                first[component][plane] = (
                    RELAX_WEIGHT * rs_ref[base + component, plane] * inv_ref[plane]
                )
        applied = [[None] * 3 for _ in range(planes)]
        for plane in range(planes):
            f = [first[k][plane] for k in range(3)]
            own = [own_ref[e, plane] for e in range(6)]
            applied[plane][0] = own[0] * f[0] + own[3] * f[1] + own[4] * f[2]
            applied[plane][1] = own[3] * f[0] + own[1] * f[1] + own[5] * f[2]
            applied[plane][2] = own[4] * f[0] + own[5] * f[1] + own[2] * f[2]
        for source in range(planes):
            for step_x in (-1, 0, 1):
                for step_y in (-1, 0, 1):
                    targets = [
                        (source - step_p, step_p)
                        for step_p in (-1, 0, 1)
                        if 0 <= source - step_p < planes and (step_p, step_x, step_y) != (0, 0, 0)
                    ]
                    if not targets:
                        continue
                    near = []
                    for component in range(3):
                        pieces = halo_pieces(base + component, source, step_x)
                        near.append(
                            neighbour_shift(first[component][source], *pieces, step_x, step_y)
                        )
                    for plane, step_p in targets:
                        direction = (step_p, step_x, step_y)
                        index = OFFSETS.index(direction)
                        projected = None
                        for component in range(3):
                            if direction[component] == 0:
                                continue
                            term = near[component]
                            if projected is None:
                                projected = term if direction[component] > 0 else -term
                            elif direction[component] > 0:
                                projected = projected + term
                            else:
                                projected = projected - term
                        along = coef_ref[1, index, plane] * projected
                        straight = coef_ref[0, index, plane]
                        for component in range(3):
                            value = applied[plane][component] - straight * near[component]
                            if direction[component] > 0:
                                value = value - along
                            elif direction[component] < 0:
                                value = value + along
                            applied[plane][component] = value
        for component in range(3):
            for plane in range(planes):
                load_tile = rs_ref[base + component, plane]
                out_ref[base + component, plane] = first[component][plane] + RELAX_WEIGHT * (
                    load_tile - applied[plane][component]
                ) * inv_ref[plane]
        return carry

    lax.fori_loop(0, loads, one_load, 0)


def smoother(sides, loads, modulus, halos):
    channels, planes, rows, cols = loads.shape
    vmem = pltpu.MemorySpace.VMEM
    return pl.pallas_call(
        smoother_kernel,
        out_shape=jax.ShapeDtypeStruct(loads.shape, jnp.float32),
        in_specs=[pl.BlockSpec(memory_space=pltpu.MemorySpace.SMEM)]
        + [pl.BlockSpec(memory_space=vmem)] * (2 + len(halos)),
        out_specs=pl.BlockSpec(memory_space=vmem),
        scratch_shapes=[
            pltpu.VMEM((2, len(OFFSETS), planes, rows, cols), jnp.float32),
            pltpu.VMEM((6, planes, rows, cols), jnp.float32),
            pltpu.VMEM((planes, rows, cols), jnp.float32),
            pltpu.VMEM((2, channels + 1, planes, cols), jnp.float32),
            pltpu.VMEM((2, channels + 1, planes, 2 * rows, cols), jnp.float32),
        ],
    )(sides, loads, modulus, *halos)


def per_device(right_sides, modulus, margin_sides, coarse_vectors, coarse_inverse):
    load_count = right_sides.shape[0]
    plane_count = right_sides.shape[2]
    row_count = right_sides.shape[3]
    column_count = right_sides.shape[4]
    cell_dims = (1, 2, 3, 4)
    partial_terms = lax.dot_general(
        coarse_vectors, right_sides, ((cell_dims, cell_dims), ((), ())), precision=lax.Precision.HIGH
    )
    restricted = butterfly_sum(partial_terms, "prow")

    loads = right_sides.reshape(load_count * 3, plane_count, row_count, column_count)
    row_first, row_last, col_first, col_last = pack(loads, modulus)
    rows_n = lax.axis_size("prow")
    cols_n = lax.axis_size("pcol")

    def line(source, axis, size, step):
        pairs = [(i, i + step) for i in range(size) if 0 <= i + step < size]
        return lax.ppermute(source, axis, pairs)

    def diagonal(source, step_row, step_col):
        pairs = []
        for a in range(rows_n):
            for b in range(cols_n):
                if 0 <= a + step_row < rows_n and 0 <= b + step_col < cols_n:
                    pairs.append((a * cols_n + b, (a + step_row) * cols_n + b + step_col))
        return lax.ppermute(source, ("prow", "pcol"), pairs)

    halos = (
        line(row_last, "prow", rows_n, 1),
        line(row_first, "prow", rows_n, -1),
        line(col_last, "pcol", cols_n, 1),
        line(col_first, "pcol", cols_n, -1),
        diagonal(col_last, 1, 1),
        diagonal(col_first, 1, -1),
        diagonal(col_last, -1, 1),
        diagonal(col_first, -1, -1),
    )
    sides = margin_sides[0, 0].astype(jnp.float32)
    smoothed = smoother(sides, loads, modulus, halos)

    solved = jnp.dot(coarse_inverse[0], restricted, precision=lax.Precision.HIGHEST)
    lifted = lax.dot_general(
        solved, coarse_vectors, (((0,), (0,)), ((), ())), precision=lax.Precision.HIGH
    )
    return smoothed.reshape(right_sides.shape) + lifted


def solution(mesh):
    in_specs = (
        P(None, None, None, "prow", "pcol"),
        P(None, "prow", "pcol"),
        P("prow", "pcol", None),
        P(None, None, None, "prow", "pcol"),
        P("pcol", None, None),
    )
    out_specs = P(None, None, None, "prow", "pcol")
    return jax.shard_map(
        per_device, mesh=mesh, in_specs=in_specs, out_specs=out_specs, check_vma=False
    )
```

```python
import jax
import jax.numpy as jnp
from jax import lax
from jax.experimental import pallas as pl
from jax.experimental.pallas import tpu as pltpu
from jax.sharding import PartitionSpec as P

RELAX_WEIGHT = 0.7
MASS_SHIFT = 0.5
DIAGONAL_SLOPE = 0.6 + 0.4 / 3.0
BOND_TOTAL = 44.0 / 3.0

OFFSETS = [
    (step_p, step_x, step_y)
    for step_p in (-1, 0, 1)
    for step_x in (-1, 0, 1)
    for step_y in (-1, 0, 1)
    if (step_p, step_x, step_y) != (0, 0, 0)
]
OWN_ENTRIES = ((0, 0), (1, 1), (2, 2), (0, 1), (0, 2), (1, 2))


def butterfly_sum(x, axis, step=1):
    size = lax.axis_size(axis)
    while step < size:
        pairs = [(i, i ^ step) for i in range(size)]
        x = x + lax.ppermute(x, axis, pairs)
        step *= 2
    return x


def neighbour_shift(tile, row_lo, row_hi, col_lo, col_hi, step_x, step_y):
    rows, cols = tile.shape
    if step_x != 0:
        rolled = pltpu.roll(tile, (-step_x) % rows, 0)
        sub = lax.broadcasted_iota(jnp.int32, tile.shape, 0)
        edge = rows - 1 if step_x > 0 else 0
        halo = row_hi if step_x > 0 else row_lo
        tile = jnp.where(sub == edge, jnp.broadcast_to(halo, tile.shape), rolled)
    if step_y != 0:
        rolled = pltpu.roll(tile, (-step_y) % cols, 1)
        lane = lax.broadcasted_iota(jnp.int32, tile.shape, 1)
        edge = cols - 1 if step_y > 0 else 0
        halo = col_hi if step_y > 0 else col_lo
        tile = jnp.where(lane == edge, jnp.broadcast_to(halo, tile.shape), rolled)
    return tile


def pack_kernel(rs_ref, mod_ref, partial_ref, row_first_ref, row_last_ref, col_first_ref, col_last_ref):
    channels, planes, rows, cols = rs_ref.shape
    count = (channels + 1) * planes
    lane = lax.broadcasted_iota(jnp.int32, (rows, cols), 1)
    tiles = col_first_ref.shape[1] // cols
    pad_from = count // rows * rows
    padding = jnp.zeros((row_first_ref.shape[0] - pad_from, cols), jnp.float32)
    row_first_ref[pl.ds(pad_from, padding.shape[0]), :] = padding
    row_last_ref[pl.ds(pad_from, padding.shape[0]), :] = padding
    first = [jnp.zeros((rows, cols), jnp.float32) for _ in range(tiles)]
    last = [jnp.zeros((rows, cols), jnp.float32) for _ in range(tiles)]
    for channel in range(channels + 1):
        for plane in range(planes):
            tile = rs_ref[channel, plane] if channel < channels else mod_ref[plane]
            j = channel * planes + plane
            row_first_ref[pl.ds(j, 1), :] = tile[0:1, :]
            row_last_ref[pl.ds(j, 1), :] = tile[rows - 1 : rows, :]
            group, place = divmod(j, cols)
            first[group] = jnp.where(lane == place, pltpu.roll(tile, place, 1), first[group])
            last[group] = jnp.where(
                lane == place, pltpu.roll(tile, (place + 1) % cols, 1), last[group]
            )
    for group in range(tiles):
        col_first_ref[:, pl.ds(group * cols, cols)] = first[group]
        col_last_ref[:, pl.ds(group * cols, cols)] = last[group]
    vectors, terms = partial_ref.shape
    start = row_first_ref.shape[0] - vectors
    row_first_ref[pl.ds(start, vectors), pl.ds(0, terms)] = partial_ref[...]
    row_last_ref[pl.ds(start, vectors), pl.ds(0, terms)] = partial_ref[...]


def pack(loads, modulus, partial):
    channels, planes, rows, cols = loads.shape
    count = (channels + 1) * planes
    lanes = -(-count // cols) * cols
    height = -(-(count + partial.shape[0]) // cols) * cols
    vmem = pltpu.MemorySpace.VMEM
    return pl.pallas_call(
        pack_kernel,
        out_shape=[
            jax.ShapeDtypeStruct((height, cols), jnp.float32),
            jax.ShapeDtypeStruct((height, cols), jnp.float32),
            jax.ShapeDtypeStruct((rows, lanes), jnp.float32),
            jax.ShapeDtypeStruct((rows, lanes), jnp.float32),
        ],
        in_specs=[pl.BlockSpec(memory_space=vmem)] * 3,
        out_specs=[pl.BlockSpec(memory_space=vmem)] * 4,
    )(loads, modulus, partial)


def edge_kernel(rlo_ref, rhi_ref, col_first_ref, col_last_ref, ext_first_ref, ext_last_ref):
    rows, lanes = col_first_ref.shape
    cols = rlo_ref.shape[1]
    low = jnp.transpose(rlo_ref[...])[:, 0:lanes]
    high = jnp.transpose(rhi_ref[...])[:, 0:lanes]
    zeros = jnp.zeros((ext_first_ref.shape[0] - rows - 2, lanes), jnp.float32)
    for out_ref, column, lane in ((ext_first_ref, col_first_ref, 0), (ext_last_ref, col_last_ref, cols - 1)):
        out_ref[pl.ds(0, 1), :] = low[lane : lane + 1, :]
        out_ref[pl.ds(1, rows), :] = column[...]
        out_ref[pl.ds(rows + 1, 1), :] = high[lane : lane + 1, :]
        out_ref[pl.ds(rows + 2, zeros.shape[0]), :] = zeros


def edges(row_lo, row_hi, col_first, col_last):
    rows, lanes = col_first.shape
    vmem = pltpu.MemorySpace.VMEM
    return pl.pallas_call(
        edge_kernel,
        out_shape=[jax.ShapeDtypeStruct((2 * rows, lanes), jnp.float32)] * 2,
        in_specs=[pl.BlockSpec(memory_space=vmem)] * 4,
        out_specs=[pl.BlockSpec(memory_space=vmem)] * 2,
    )(row_lo, row_hi, col_first, col_last)


def smoother_kernel(
    sides_ref, rs_ref, mod_ref, rlo_ref, rhi_ref, clo_ref, chi_ref,
    out_ref, coef_ref, own_ref, inv_ref, row_ref, col_ref,
):
    channels, planes, rows, cols = rs_ref.shape
    loads = channels // 3
    mod_channel = channels
    shape = (rows, cols)
    sub = lax.broadcasted_iota(jnp.int32, shape, 0)
    lane = lax.broadcasted_iota(jnp.int32, shape, 1)
    one = jnp.ones(shape, jnp.float32)
    factor_x = {
        -1: jnp.where(sub == 0, sides_ref[0], one),
        0: None,
        1: jnp.where(sub == rows - 1, sides_ref[1], one),
    }
    factor_y = {
        -1: jnp.where(lane == 0, sides_ref[2], one),
        0: None,
        1: jnp.where(lane == cols - 1, sides_ref[3], one),
    }

    def halo_pieces(channel, plane, step_x):
        row_lo = row_ref[0, channel, pl.ds(plane, 1), :]
        row_hi = row_ref[1, channel, pl.ds(plane, 1), :]
        col_lo = col_ref[0, channel, plane, pl.ds(1 + step_x, rows), :]
        col_hi = col_ref[1, channel, plane, pl.ds(1 + step_x, rows), :]
        return row_lo, row_hi, col_lo, col_hi

    for channel in range(channels + 1):
        row_ref[0, channel] = rlo_ref[pl.ds(channel * planes, planes), :]
        row_ref[1, channel] = rhi_ref[pl.ds(channel * planes, planes), :]
        for plane in range(planes):
            j = channel * planes + plane
            group, place = divmod(j, cols)
            window = pl.ds(group * cols, cols)
            for side, (edge, column) in enumerate(((0, clo_ref), (cols - 1, chi_ref))):
                col_ref[side, channel, plane] = pltpu.roll(
                    column[:, window], (edge - place) % cols, 1
                )
    row_inverse = RELAX_WEIGHT / (MASS_SHIFT + DIAGONAL_SLOPE * row_ref[:, mod_channel : mod_channel + 1])
    row_ref[:, 0:channels] = row_ref[:, 0:channels] * row_inverse
    col_inverse = RELAX_WEIGHT / (MASS_SHIFT + DIAGONAL_SLOPE * col_ref[:, mod_channel : mod_channel + 1, :, 0 : rows + 2])
    col_ref[:, 0:channels, :, 0 : rows + 2] = col_ref[:, 0:channels, :, 0 : rows + 2] * col_inverse

    for plane in range(planes):
        own_modulus = mod_ref[plane]
        inv_ref[plane] = 1.0 / (MASS_SHIFT + DIAGONAL_SLOPE * own_modulus)
        own = [None] * 6
        for index, (step_p, step_x, step_y) in enumerate(OFFSETS):
            source = plane + step_p
            length = step_p * step_p + step_x * step_x + step_y * step_y
            weight = 1.0 / (length * BOND_TOTAL)
            if 0 <= source < planes:
                pieces = halo_pieces(mod_channel, source, step_x)
                near_modulus = neighbour_shift(mod_ref[source], *pieces, step_x, step_y)
                bond = (0.5 * weight) * (own_modulus + near_modulus)
                coefficient = bond
                if factor_x[step_x] is not None:
                    coefficient = coefficient * factor_x[step_x]
                if factor_y[step_y] is not None:
                    coefficient = coefficient * factor_y[step_y]
                coef_ref[0, index, plane] = 0.6 * coefficient
                coef_ref[1, index, plane] = (0.4 / length) * coefficient
            else:
                bond = (0.5 * weight) * own_modulus
            direction = (step_p, step_x, step_y)
            for entry, (a, b) in enumerate(OWN_ENTRIES):
                scale = 0.4 * direction[a] * direction[b] / length
                if a == b:
                    scale += 0.6
                if scale == 0.0:
                    continue
                term = scale * bond
                own[entry] = term if own[entry] is None else own[entry] + term
        for entry, (a, b) in enumerate(OWN_ENTRIES):
            value = own[entry]
            if a == b:
                value = value + MASS_SHIFT
            own_ref[entry, plane] = value

    def one_load(load, carry):
        base = load * 3
        first = [[None] * planes for _ in range(3)]
        for component in range(3):
            for plane in range(planes):
                first[component][plane] = (
                    RELAX_WEIGHT * rs_ref[base + component, plane] * inv_ref[plane]
                )
        applied = [[None] * 3 for _ in range(planes)]
        for plane in range(planes):
            f = [first[k][plane] for k in range(3)]
            own = [own_ref[e, plane] for e in range(6)]
            applied[plane][0] = own[0] * f[0] + own[3] * f[1] + own[4] * f[2]
            applied[plane][1] = own[3] * f[0] + own[1] * f[1] + own[5] * f[2]
            applied[plane][2] = own[4] * f[0] + own[5] * f[1] + own[2] * f[2]
        for source in range(planes):
            for step_x in (-1, 0, 1):
                for step_y in (-1, 0, 1):
                    targets = [
                        (source - step_p, step_p)
                        for step_p in (-1, 0, 1)
                        if 0 <= source - step_p < planes and (step_p, step_x, step_y) != (0, 0, 0)
                    ]
                    if not targets:
                        continue
                    near = []
                    for component in range(3):
                        pieces = halo_pieces(base + component, source, step_x)
                        near.append(
                            neighbour_shift(first[component][source], *pieces, step_x, step_y)
                        )
                    for plane, step_p in targets:
                        direction = (step_p, step_x, step_y)
                        index = OFFSETS.index(direction)
                        projected = None
                        for component in range(3):
                            if direction[component] == 0:
                                continue
                            term = near[component]
                            if projected is None:
                                projected = term if direction[component] > 0 else -term
                            elif direction[component] > 0:
                                projected = projected + term
                            else:
                                projected = projected - term
                        along = coef_ref[1, index, plane] * projected
                        straight = coef_ref[0, index, plane]
                        for component in range(3):
                            value = applied[plane][component] - straight * near[component]
                            if direction[component] > 0:
                                value = value - along
                            elif direction[component] < 0:
                                value = value + along
                            applied[plane][component] = value
        for component in range(3):
            for plane in range(planes):
                load_tile = rs_ref[base + component, plane]
                out_ref[base + component, plane] = first[component][plane] + RELAX_WEIGHT * (
                    load_tile - applied[plane][component]
                ) * inv_ref[plane]
        return carry

    lax.fori_loop(0, loads, one_load, 0)


def smoother(sides, loads, modulus, halos):
    channels, planes, rows, cols = loads.shape
    vmem = pltpu.MemorySpace.VMEM
    return pl.pallas_call(
        smoother_kernel,
        out_shape=jax.ShapeDtypeStruct(loads.shape, jnp.float32),
        in_specs=[pl.BlockSpec(memory_space=pltpu.MemorySpace.SMEM)]
        + [pl.BlockSpec(memory_space=vmem)] * (2 + len(halos)),
        out_specs=pl.BlockSpec(memory_space=vmem),
        scratch_shapes=[
            pltpu.VMEM((2, len(OFFSETS), planes, rows, cols), jnp.float32),
            pltpu.VMEM((6, planes, rows, cols), jnp.float32),
            pltpu.VMEM((planes, rows, cols), jnp.float32),
            pltpu.VMEM((2, channels + 1, planes, cols), jnp.float32),
            pltpu.VMEM((2, channels + 1, planes, 2 * rows, cols), jnp.float32),
        ],
    )(sides, loads, modulus, *halos)


def per_device(right_sides, modulus, margin_sides, coarse_vectors, coarse_inverse):
    load_count = right_sides.shape[0]
    plane_count = right_sides.shape[2]
    row_count = right_sides.shape[3]
    column_count = right_sides.shape[4]
    cell_dims = (1, 2, 3, 4)
    partial_terms = lax.dot_general(
        coarse_vectors, right_sides, ((cell_dims, cell_dims), ((), ())), precision=lax.Precision.HIGHEST
    )

    loads = right_sides.reshape(load_count * 3, plane_count, row_count, column_count)
    row_first, row_last, col_first, col_last = pack(loads, modulus, partial_terms)
    rows_n = lax.axis_size("prow")
    cols_n = lax.axis_size("pcol")

    def line(source, axis, size, step):
        pairs = [(i, i + step) for i in range(size) if 0 <= i + step < size]
        return lax.ppermute(source, axis, pairs)

    row_lo = line(row_last, "prow", rows_n, 1)
    row_hi = line(row_first, "prow", rows_n, -1)
    vectors, terms = partial_terms.shape
    even = lax.axis_index("prow") % 2 == 0
    partner = jnp.where(even, row_hi[-vectors:, :terms], row_lo[-vectors:, :terms])
    restricted = butterfly_sum(partial_terms + partner, "prow", 2)
    ext_first, ext_last = edges(row_lo, row_hi, col_first, col_last)
    halos = (
        row_lo,
        row_hi,
        line(ext_last, "pcol", cols_n, 1),
        line(ext_first, "pcol", cols_n, -1),
    )
    sides = margin_sides[0, 0].astype(jnp.float32)
    smoothed = smoother(sides, loads, modulus, halos)

    solved = jnp.dot(coarse_inverse[0], restricted, precision=lax.Precision.HIGHEST)
    lifted = lax.dot_general(
        solved, coarse_vectors, (((0,), (0,)), ((), ())), precision=lax.Precision.HIGHEST
    )
    return smoothed.reshape(right_sides.shape) + lifted


def solution(mesh):
    in_specs = (
        P(None, None, None, "prow", "pcol"),
        P(None, "prow", "pcol"),
        P("prow", "pcol", None),
        P(None, None, None, "prow", "pcol"),
        P("pcol", None, None),
    )
    out_specs = P(None, None, None, "prow", "pcol")
    return jax.shard_map(
        per_device, mesh=mesh, in_specs=in_specs, out_specs=out_specs, check_vma=False
    )
```

```python
import jax
import jax.numpy as jnp
from jax import lax
from jax.experimental import pallas as pl
from jax.experimental.pallas import tpu as pltpu
from jax.sharding import PartitionSpec as P


RELAX_WEIGHT = 0.7
MASS_SHIFT = 0.5
DIAGONAL_SLOPE = 0.6 + 0.4 / 3.0
BOND_TOTAL = 44.0 / 3.0

OFFSETS = [
    (step_p, step_x, step_y)
    for step_p in (-1, 0, 1)
    for step_x in (-1, 0, 1)
    for step_y in (-1, 0, 1)
    if (step_p, step_x, step_y) != (0, 0, 0)
]
OWN_ENTRIES = ((0, 0), (1, 1), (2, 2), (0, 1), (0, 2), (1, 2))


def butterfly_sum(x, axis, step=1):
    size = lax.axis_size(axis)
    while step < size:
        pairs = [(i, i ^ step) for i in range(size)]
        x = x + lax.ppermute(x, axis, pairs)
        step *= 2
    return x


def neighbour_shift(tile, row_lo, row_hi, col_lo, col_hi, step_x, step_y):
    rows, cols = tile.shape
    if step_x != 0:
        rolled = pltpu.roll(tile, (-step_x) % rows, 0)
        sub = lax.broadcasted_iota(jnp.int32, tile.shape, 0)
        edge = rows - 1 if step_x > 0 else 0
        halo = row_hi if step_x > 0 else row_lo
        tile = jnp.where(sub == edge, jnp.broadcast_to(halo, tile.shape), rolled)
    if step_y != 0:
        rolled = pltpu.roll(tile, (-step_y) % cols, 1)
        lane = lax.broadcasted_iota(jnp.int32, tile.shape, 1)
        edge = cols - 1 if step_y > 0 else 0
        halo = col_hi if step_y > 0 else col_lo
        tile = jnp.where(lane == edge, jnp.broadcast_to(halo, tile.shape), rolled)
    return tile


def pack_kernel(rs_ref, mod_ref, partial_ref, row_first_ref, row_last_ref, col_first_ref, col_last_ref):
    channels, planes, rows, cols = rs_ref.shape
    count = (channels + 1) * planes
    lane = lax.broadcasted_iota(jnp.int32, (rows, cols), 1)
    tiles = col_first_ref.shape[1] // cols
    pad_from = count // rows * rows
    padding = jnp.zeros((row_first_ref.shape[0] - pad_from, cols), jnp.float32)
    row_first_ref[pl.ds(pad_from, padding.shape[0]), :] = padding
    row_last_ref[pl.ds(pad_from, padding.shape[0]), :] = padding
    first = [jnp.zeros((rows, cols), jnp.float32) for _ in range(tiles)]
    last = [jnp.zeros((rows, cols), jnp.float32) for _ in range(tiles)]
    for channel in range(channels + 1):
        for plane in range(planes):
            tile = rs_ref[channel, plane] if channel < channels else mod_ref[plane]
            j = channel * planes + plane
            row_first_ref[pl.ds(j, 1), :] = tile[0:1, :]
            row_last_ref[pl.ds(j, 1), :] = tile[rows - 1 : rows, :]
            group, place = divmod(j, cols)
            first[group] = jnp.where(lane == place, pltpu.roll(tile, place, 1), first[group])
            last[group] = jnp.where(
                lane == place, pltpu.roll(tile, (place + 1) % cols, 1), last[group]
            )
    for group in range(tiles):
        col_first_ref[:, pl.ds(group * cols, cols)] = first[group]
        col_last_ref[:, pl.ds(group * cols, cols)] = last[group]
    vectors, terms = partial_ref.shape
    start = row_first_ref.shape[0] - vectors
    row_first_ref[pl.ds(start, vectors), pl.ds(0, terms)] = partial_ref[...]
    row_last_ref[pl.ds(start, vectors), pl.ds(0, terms)] = partial_ref[...]


def pack(loads, modulus, partial):
    channels, planes, rows, cols = loads.shape
    count = (channels + 1) * planes
    lanes = -(-count // cols) * cols
    height = -(-(count + partial.shape[0]) // cols) * cols
    vmem = pltpu.MemorySpace.VMEM
    return pl.pallas_call(
        pack_kernel,
        out_shape=[
            jax.ShapeDtypeStruct((height, cols), jnp.float32),
            jax.ShapeDtypeStruct((height, cols), jnp.float32),
            jax.ShapeDtypeStruct((rows, lanes), jnp.float32),
            jax.ShapeDtypeStruct((rows, lanes), jnp.float32),
        ],
        in_specs=[pl.BlockSpec(memory_space=vmem)] * 3,
        out_specs=[pl.BlockSpec(memory_space=vmem)] * 4,
    )(loads, modulus, partial)


def edge_kernel(rlo_ref, rhi_ref, col_first_ref, col_last_ref, ext_first_ref, ext_last_ref):
    rows, lanes = col_first_ref.shape
    cols = rlo_ref.shape[1]
    low = jnp.transpose(rlo_ref[...])[:, 0:lanes]
    high = jnp.transpose(rhi_ref[...])[:, 0:lanes]
    zeros = jnp.zeros((ext_first_ref.shape[0] - rows - 2, lanes), jnp.float32)
    for out_ref, column, lane in ((ext_first_ref, col_first_ref, 0), (ext_last_ref, col_last_ref, cols - 1)):
        out_ref[pl.ds(0, 1), :] = low[lane : lane + 1, :]
        out_ref[pl.ds(1, rows), :] = column[...]
        out_ref[pl.ds(rows + 1, 1), :] = high[lane : lane + 1, :]
        out_ref[pl.ds(rows + 2, zeros.shape[0]), :] = zeros


def edges(row_lo, row_hi, col_first, col_last):
    rows, lanes = col_first.shape
    vmem = pltpu.MemorySpace.VMEM
    return pl.pallas_call(
        edge_kernel,
        out_shape=[jax.ShapeDtypeStruct((2 * rows, lanes), jnp.float32)] * 2,
        in_specs=[pl.BlockSpec(memory_space=vmem)] * 4,
        out_specs=[pl.BlockSpec(memory_space=vmem)] * 2,
    )(row_lo, row_hi, col_first, col_last)


def smoother_kernel(
    sides_ref, rs_ref, mod_ref, rlo_ref, rhi_ref, clo_ref, chi_ref,
    out_ref, coef_ref, own_ref, inv_ref, row_ref, col_ref,
):
    channels, planes, rows, cols = rs_ref.shape
    loads = channels // 3
    mod_channel = channels
    shape = (rows, cols)
    sub = lax.broadcasted_iota(jnp.int32, shape, 0)
    lane = lax.broadcasted_iota(jnp.int32, shape, 1)
    one = jnp.ones(shape, jnp.float32)
    factor_x = {
        -1: jnp.where(sub == 0, sides_ref[0], one),
        0: None,
        1: jnp.where(sub == rows - 1, sides_ref[1], one),
    }
    factor_y = {
        -1: jnp.where(lane == 0, sides_ref[2], one),
        0: None,
        1: jnp.where(lane == cols - 1, sides_ref[3], one),
    }

    def halo_pieces(channel, plane, step_x):
        row_lo = row_ref[0, channel, pl.ds(plane, 1), :]
        row_hi = row_ref[1, channel, pl.ds(plane, 1), :]
        col_lo = col_ref[0, channel, plane, pl.ds(1 + step_x, rows), :]
        col_hi = col_ref[1, channel, plane, pl.ds(1 + step_x, rows), :]
        return row_lo, row_hi, col_lo, col_hi

    for channel in range(channels + 1):
        row_ref[0, channel] = rlo_ref[pl.ds(channel * planes, planes), :]
        row_ref[1, channel] = rhi_ref[pl.ds(channel * planes, planes), :]
        for plane in range(planes):
            j = channel * planes + plane
            group, place = divmod(j, cols)
            window = pl.ds(group * cols, cols)
            for side, (edge, column) in enumerate(((0, clo_ref), (cols - 1, chi_ref))):
                col_ref[side, channel, plane] = pltpu.roll(
                    column[:, window], (edge - place) % cols, 1
                )
    row_inverse = RELAX_WEIGHT / (MASS_SHIFT + DIAGONAL_SLOPE * row_ref[:, mod_channel : mod_channel + 1])
    row_ref[:, 0:channels] = row_ref[:, 0:channels] * row_inverse
    col_inverse = RELAX_WEIGHT / (MASS_SHIFT + DIAGONAL_SLOPE * col_ref[:, mod_channel : mod_channel + 1, :, 0 : rows + 2])
    col_ref[:, 0:channels, :, 0 : rows + 2] = col_ref[:, 0:channels, :, 0 : rows + 2] * col_inverse

    for plane in range(planes):
        own_modulus = mod_ref[plane]
        inv_ref[plane] = 1.0 / (MASS_SHIFT + DIAGONAL_SLOPE * own_modulus)
        own = [None] * 6
        for index, (step_p, step_x, step_y) in enumerate(OFFSETS):
            source = plane + step_p
            length = step_p * step_p + step_x * step_x + step_y * step_y
            weight = 1.0 / (length * BOND_TOTAL)
            if 0 <= source < planes:
                pieces = halo_pieces(mod_channel, source, step_x)
                near_modulus = neighbour_shift(mod_ref[source], *pieces, step_x, step_y)
                bond = (0.5 * weight) * (own_modulus + near_modulus)
                coefficient = bond
                if factor_x[step_x] is not None:
                    coefficient = coefficient * factor_x[step_x]
                if factor_y[step_y] is not None:
                    coefficient = coefficient * factor_y[step_y]
                coef_ref[0, index, plane] = 0.6 * coefficient
                coef_ref[1, index, plane] = (0.4 / length) * coefficient
            else:
                bond = (0.5 * weight) * own_modulus
            direction = (step_p, step_x, step_y)
            for entry, (a, b) in enumerate(OWN_ENTRIES):
                scale = 0.4 * direction[a] * direction[b] / length
                if a == b:
                    scale += 0.6
                if scale == 0.0:
                    continue
                term = scale * bond
                own[entry] = term if own[entry] is None else own[entry] + term
        for entry, (a, b) in enumerate(OWN_ENTRIES):
            value = own[entry]
            if a == b:
                value = value + MASS_SHIFT
            own_ref[entry, plane] = value

    def one_load(load, carry):
        base = load * 3
        first = [[None] * planes for _ in range(3)]
        for component in range(3):
            for plane in range(planes):
                first[component][plane] = (
                    RELAX_WEIGHT * rs_ref[base + component, plane] * inv_ref[plane]
                )
        applied = [[None] * 3 for _ in range(planes)]
        for plane in range(planes):
            f = [first[k][plane] for k in range(3)]
            own = [own_ref[e, plane] for e in range(6)]
            applied[plane][0] = own[0] * f[0] + own[3] * f[1] + own[4] * f[2]
            applied[plane][1] = own[3] * f[0] + own[1] * f[1] + own[5] * f[2]
            applied[plane][2] = own[4] * f[0] + own[5] * f[1] + own[2] * f[2]
        for source in range(planes):
            for step_x in (-1, 0, 1):
                for step_y in (-1, 0, 1):
                    targets = [
                        (source - step_p, step_p)
                        for step_p in (-1, 0, 1)
                        if 0 <= source - step_p < planes and (step_p, step_x, step_y) != (0, 0, 0)
                    ]
                    if not targets:
                        continue
                    near = []
                    for component in range(3):
                        pieces = halo_pieces(base + component, source, step_x)
                        near.append(
                            neighbour_shift(first[component][source], *pieces, step_x, step_y)
                        )
                    for plane, step_p in targets:
                        direction = (step_p, step_x, step_y)
                        index = OFFSETS.index(direction)
                        projected = None
                        for component in range(3):
                            if direction[component] == 0:
                                continue
                            term = near[component]
                            if projected is None:
                                projected = term if direction[component] > 0 else -term
                            elif direction[component] > 0:
                                projected = projected + term
                            else:
                                projected = projected - term
                        along = coef_ref[1, index, plane] * projected
                        straight = coef_ref[0, index, plane]
                        for component in range(3):
                            value = applied[plane][component] - straight * near[component]
                            if direction[component] > 0:
                                value = value - along
                            elif direction[component] < 0:
                                value = value + along
                            applied[plane][component] = value
        for component in range(3):
            for plane in range(planes):
                load_tile = rs_ref[base + component, plane]
                out_ref[base + component, plane] = first[component][plane] + RELAX_WEIGHT * (
                    load_tile - applied[plane][component]
                ) * inv_ref[plane]
        return carry

    lax.fori_loop(0, loads, one_load, 0)


def smoother(sides, loads, modulus, halos):
    channels, planes, rows, cols = loads.shape
    vmem = pltpu.MemorySpace.VMEM
    return pl.pallas_call(
        smoother_kernel,
        out_shape=jax.ShapeDtypeStruct(loads.shape, jnp.float32),
        in_specs=[pl.BlockSpec(memory_space=pltpu.MemorySpace.SMEM)]
        + [pl.BlockSpec(memory_space=vmem)] * (2 + len(halos)),
        out_specs=pl.BlockSpec(memory_space=vmem),
        scratch_shapes=[
            pltpu.VMEM((2, len(OFFSETS), planes, rows, cols), jnp.float32),
            pltpu.VMEM((6, planes, rows, cols), jnp.float32),
            pltpu.VMEM((planes, rows, cols), jnp.float32),
            pltpu.VMEM((2, channels + 1, planes, cols), jnp.float32),
            pltpu.VMEM((2, channels + 1, planes, 2 * rows, cols), jnp.float32),
        ],
    )(sides, loads, modulus, *halos)


def per_device_body(right_sides, modulus, margin_sides, coarse_vectors, coarse_inverse):
    load_count = right_sides.shape[0]
    plane_count = right_sides.shape[2]
    row_count = right_sides.shape[3]
    column_count = right_sides.shape[4]
    cell_dims = (1, 2, 3, 4)
    partial_terms = lax.dot_general(
        coarse_vectors, right_sides, ((cell_dims, cell_dims), ((), ())), precision=lax.Precision.HIGHEST
    )

    loads = right_sides.reshape(load_count * 3, plane_count, row_count, column_count)
    row_first, row_last, col_first, col_last = pack(loads, modulus, partial_terms)
    rows_n = lax.axis_size("prow")
    cols_n = lax.axis_size("pcol")

    def line(source, axis, size, step):
        pairs = [(i, i + step) for i in range(size) if 0 <= i + step < size]
        return lax.ppermute(source, axis, pairs)

    row_lo = line(row_last, "prow", rows_n, 1)
    row_hi = line(row_first, "prow", rows_n, -1)
    vectors, terms = partial_terms.shape
    even = lax.axis_index("prow") % 2 == 0
    partner = jnp.where(even, row_hi[-vectors:, :terms], row_lo[-vectors:, :terms])
    restricted = butterfly_sum(partial_terms + partner, "prow", 2)
    ext_first, ext_last = edges(row_lo, row_hi, col_first, col_last)
    halos = (row_lo, row_hi, line(ext_last, "pcol", cols_n, 1), line(ext_first, "pcol", cols_n, -1))
    sides = margin_sides[0, 0].astype(jnp.float32)
    smoothed = smoother(sides, loads, modulus, halos)

    solved = jnp.dot(coarse_inverse[0], restricted, precision=lax.Precision.HIGHEST)
    lifted = lax.dot_general(
        solved, coarse_vectors, (((0,), (0,)), ((), ())), precision=lax.Precision.HIGHEST
    )
    return smoothed.reshape(right_sides.shape) + lifted


def solution(mesh):
    in_specs = (
        P(None, None, None, "prow", "pcol"),
        P(None, "prow", "pcol"),
        P("prow", "pcol", None),
        P(None, None, None, "prow", "pcol"),
        P("pcol", None, None),
    )
    out_specs = P(None, None, None, "prow", "pcol")
    return jax.shard_map(
        per_device_body, mesh=mesh, in_specs=in_specs, out_specs=out_specs, check_vma=False
    )
```

```python
import jax
import jax.numpy as jnp
from jax import lax
from jax.experimental import pallas as pl
from jax.experimental.pallas import tpu as pltpu
from jax.sharding import PartitionSpec as P


RELAX_WEIGHT = 0.7
MASS_SHIFT = 0.5
DIAGONAL_SLOPE = 0.6 + 0.4 / 3.0
BOND_TOTAL = 44.0 / 3.0

OFFSETS = [
    (step_p, step_x, step_y)
    for step_p in (-1, 0, 1)
    for step_x in (-1, 0, 1)
    for step_y in (-1, 0, 1)
    if (step_p, step_x, step_y) != (0, 0, 0)
]
OWN_ENTRIES = ((0, 0), (1, 1), (2, 2), (0, 1), (0, 2), (1, 2))


def butterfly_sum(x, axis, step=1, after_first=None):
    size = lax.axis_size(axis)
    while step < size:
        pairs = [(i, i ^ step) for i in range(size)]
        x = x + lax.ppermute(x, axis, pairs)
        if after_first is not None:
            x, after_first = lax.optimization_barrier((x, after_first()))
            held = after_first
            after_first = None
        step *= 2
    return x, held


def neighbour_shift(tile, row_lo, row_hi, col_lo, col_hi, step_x, step_y):
    rows, cols = tile.shape
    if step_x != 0:
        rolled = pltpu.roll(tile, (-step_x) % rows, 0)
        sub = lax.broadcasted_iota(jnp.int32, tile.shape, 0)
        edge = rows - 1 if step_x > 0 else 0
        halo = row_hi if step_x > 0 else row_lo
        tile = jnp.where(sub == edge, jnp.broadcast_to(halo, tile.shape), rolled)
    if step_y != 0:
        rolled = pltpu.roll(tile, (-step_y) % cols, 1)
        lane = lax.broadcasted_iota(jnp.int32, tile.shape, 1)
        edge = cols - 1 if step_y > 0 else 0
        halo = col_hi if step_y > 0 else col_lo
        tile = jnp.where(lane == edge, jnp.broadcast_to(halo, tile.shape), rolled)
    return tile


def pack_kernel(rs_ref, mod_ref, partial_ref, row_first_ref, row_last_ref, col_first_ref, col_last_ref):
    channels, planes, rows, cols = rs_ref.shape
    count = (channels + 1) * planes
    lane = lax.broadcasted_iota(jnp.int32, (rows, cols), 1)
    tiles = col_first_ref.shape[1] // cols
    pad_from = count // rows * rows
    padding = jnp.zeros((row_first_ref.shape[0] - pad_from, cols), jnp.float32)
    row_first_ref[pl.ds(pad_from, padding.shape[0]), :] = padding
    row_last_ref[pl.ds(pad_from, padding.shape[0]), :] = padding
    first = [jnp.zeros((rows, cols), jnp.float32) for _ in range(tiles)]
    last = [jnp.zeros((rows, cols), jnp.float32) for _ in range(tiles)]
    for channel in range(channels + 1):
        for plane in range(planes):
            tile = rs_ref[channel, plane] if channel < channels else mod_ref[plane]
            j = channel * planes + plane
            row_first_ref[pl.ds(j, 1), :] = tile[0:1, :]
            row_last_ref[pl.ds(j, 1), :] = tile[rows - 1 : rows, :]
            group, place = divmod(j, cols)
            first[group] = jnp.where(lane == place, pltpu.roll(tile, place, 1), first[group])
            last[group] = jnp.where(
                lane == place, pltpu.roll(tile, (place + 1) % cols, 1), last[group]
            )
    for group in range(tiles):
        col_first_ref[:, pl.ds(group * cols, cols)] = first[group]
        col_last_ref[:, pl.ds(group * cols, cols)] = last[group]
    vectors, terms = partial_ref.shape
    start = row_first_ref.shape[0] - vectors
    row_first_ref[pl.ds(start, vectors), pl.ds(0, terms)] = partial_ref[...]
    row_last_ref[pl.ds(start, vectors), pl.ds(0, terms)] = partial_ref[...]


def pack(loads, modulus, partial):
    channels, planes, rows, cols = loads.shape
    count = (channels + 1) * planes
    lanes = -(-count // cols) * cols
    height = -(-(count + partial.shape[0]) // cols) * cols
    vmem = pltpu.MemorySpace.VMEM
    return pl.pallas_call(
        pack_kernel,
        out_shape=[
            jax.ShapeDtypeStruct((height, cols), jnp.float32),
            jax.ShapeDtypeStruct((height, cols), jnp.float32),
            jax.ShapeDtypeStruct((rows, lanes), jnp.float32),
            jax.ShapeDtypeStruct((rows, lanes), jnp.float32),
        ],
        in_specs=[pl.BlockSpec(memory_space=vmem)] * 3,
        out_specs=[pl.BlockSpec(memory_space=vmem)] * 4,
    )(loads, modulus, partial)


def edge_kernel(rlo_ref, rhi_ref, col_first_ref, col_last_ref, ext_first_ref, ext_last_ref):
    rows, lanes = col_first_ref.shape
    cols = rlo_ref.shape[1]
    low = jnp.transpose(rlo_ref[...])[:, 0:lanes]
    high = jnp.transpose(rhi_ref[...])[:, 0:lanes]
    zeros = jnp.zeros((ext_first_ref.shape[0] - rows - 2, lanes), jnp.float32)
    for out_ref, column, lane in ((ext_first_ref, col_first_ref, 0), (ext_last_ref, col_last_ref, cols - 1)):
        out_ref[pl.ds(0, 1), :] = low[lane : lane + 1, :]
        out_ref[pl.ds(1, rows), :] = column[...]
        out_ref[pl.ds(rows + 1, 1), :] = high[lane : lane + 1, :]
        out_ref[pl.ds(rows + 2, zeros.shape[0]), :] = zeros


def edges(row_lo, row_hi, col_first, col_last):
    rows, lanes = col_first.shape
    vmem = pltpu.MemorySpace.VMEM
    return pl.pallas_call(
        edge_kernel,
        out_shape=[jax.ShapeDtypeStruct((2 * rows, lanes), jnp.float32)] * 2,
        in_specs=[pl.BlockSpec(memory_space=vmem)] * 4,
        out_specs=[pl.BlockSpec(memory_space=vmem)] * 2,
    )(row_lo, row_hi, col_first, col_last)


def smoother_kernel(
    sides_ref, rs_ref, mod_ref, rlo_ref, rhi_ref, clo_ref, chi_ref,
    out_ref, coef_ref, own_ref, inv_ref, row_ref, col_ref,
):
    channels, planes, rows, cols = rs_ref.shape
    loads = channels // 3
    mod_channel = channels
    shape = (rows, cols)
    sub = lax.broadcasted_iota(jnp.int32, shape, 0)
    lane = lax.broadcasted_iota(jnp.int32, shape, 1)
    one = jnp.ones(shape, jnp.float32)
    factor_x = {
        -1: jnp.where(sub == 0, sides_ref[0], one),
        0: None,
        1: jnp.where(sub == rows - 1, sides_ref[1], one),
    }
    factor_y = {
        -1: jnp.where(lane == 0, sides_ref[2], one),
        0: None,
        1: jnp.where(lane == cols - 1, sides_ref[3], one),
    }

    def halo_pieces(channel, plane, step_x):
        row_lo = row_ref[0, channel, pl.ds(plane, 1), :]
        row_hi = row_ref[1, channel, pl.ds(plane, 1), :]
        col_lo = col_ref[0, channel, plane, pl.ds(1 + step_x, rows), :]
        col_hi = col_ref[1, channel, plane, pl.ds(1 + step_x, rows), :]
        return row_lo, row_hi, col_lo, col_hi

    for channel in range(channels + 1):
        row_ref[0, channel] = rlo_ref[pl.ds(channel * planes, planes), :]
        row_ref[1, channel] = rhi_ref[pl.ds(channel * planes, planes), :]
        for plane in range(planes):
            j = channel * planes + plane
            group, place = divmod(j, cols)
            window = pl.ds(group * cols, cols)
            for side, (edge, column) in enumerate(((0, clo_ref), (cols - 1, chi_ref))):
                col_ref[side, channel, plane] = pltpu.roll(
                    column[:, window], (edge - place) % cols, 1
                )
    row_inverse = RELAX_WEIGHT / (MASS_SHIFT + DIAGONAL_SLOPE * row_ref[:, mod_channel : mod_channel + 1])
    row_ref[:, 0:channels] = row_ref[:, 0:channels] * row_inverse
    col_inverse = RELAX_WEIGHT / (MASS_SHIFT + DIAGONAL_SLOPE * col_ref[:, mod_channel : mod_channel + 1, :, 0 : rows + 2])
    col_ref[:, 0:channels, :, 0 : rows + 2] = col_ref[:, 0:channels, :, 0 : rows + 2] * col_inverse

    for plane in range(planes):
        own_modulus = mod_ref[plane]
        inv_ref[plane] = 1.0 / (MASS_SHIFT + DIAGONAL_SLOPE * own_modulus)
        own = [None] * 6
        for index, (step_p, step_x, step_y) in enumerate(OFFSETS):
            source = plane + step_p
            length = step_p * step_p + step_x * step_x + step_y * step_y
            weight = 1.0 / (length * BOND_TOTAL)
            if 0 <= source < planes:
                pieces = halo_pieces(mod_channel, source, step_x)
                near_modulus = neighbour_shift(mod_ref[source], *pieces, step_x, step_y)
                bond = (0.5 * weight) * (own_modulus + near_modulus)
                coefficient = bond
                if factor_x[step_x] is not None:
                    coefficient = coefficient * factor_x[step_x]
                if factor_y[step_y] is not None:
                    coefficient = coefficient * factor_y[step_y]
                coef_ref[0, index, plane] = 0.6 * coefficient
                coef_ref[1, index, plane] = (0.4 / length) * coefficient
            else:
                bond = (0.5 * weight) * own_modulus
            direction = (step_p, step_x, step_y)
            for entry, (a, b) in enumerate(OWN_ENTRIES):
                scale = 0.4 * direction[a] * direction[b] / length
                if a == b:
                    scale += 0.6
                if scale == 0.0:
                    continue
                term = scale * bond
                own[entry] = term if own[entry] is None else own[entry] + term
        for entry, (a, b) in enumerate(OWN_ENTRIES):
            value = own[entry]
            if a == b:
                value = value + MASS_SHIFT
            own_ref[entry, plane] = value

    def one_load(load, carry):
        base = load * 3
        first = [[None] * planes for _ in range(3)]
        for component in range(3):
            for plane in range(planes):
                first[component][plane] = (
                    RELAX_WEIGHT * rs_ref[base + component, plane] * inv_ref[plane]
                )
        applied = [[None] * 3 for _ in range(planes)]
        for plane in range(planes):
            f = [first[k][plane] for k in range(3)]
            own = [own_ref[e, plane] for e in range(6)]
            applied[plane][0] = own[0] * f[0] + own[3] * f[1] + own[4] * f[2]
            applied[plane][1] = own[3] * f[0] + own[1] * f[1] + own[5] * f[2]
            applied[plane][2] = own[4] * f[0] + own[5] * f[1] + own[2] * f[2]
        for source in range(planes):
            for step_x in (-1, 0, 1):
                for step_y in (-1, 0, 1):
                    targets = [
                        (source - step_p, step_p)
                        for step_p in (-1, 0, 1)
                        if 0 <= source - step_p < planes and (step_p, step_x, step_y) != (0, 0, 0)
                    ]
                    if not targets:
                        continue
                    near = []
                    for component in range(3):
                        pieces = halo_pieces(base + component, source, step_x)
                        near.append(
                            neighbour_shift(first[component][source], *pieces, step_x, step_y)
                        )
                    for plane, step_p in targets:
                        direction = (step_p, step_x, step_y)
                        index = OFFSETS.index(direction)
                        projected = None
                        for component in range(3):
                            if direction[component] == 0:
                                continue
                            term = near[component]
                            if projected is None:
                                projected = term if direction[component] > 0 else -term
                            elif direction[component] > 0:
                                projected = projected + term
                            else:
                                projected = projected - term
                        along = coef_ref[1, index, plane] * projected
                        straight = coef_ref[0, index, plane]
                        for component in range(3):
                            value = applied[plane][component] - straight * near[component]
                            if direction[component] > 0:
                                value = value - along
                            elif direction[component] < 0:
                                value = value + along
                            applied[plane][component] = value
        for component in range(3):
            for plane in range(planes):
                load_tile = rs_ref[base + component, plane]
                out_ref[base + component, plane] = first[component][plane] + RELAX_WEIGHT * (
                    load_tile - applied[plane][component]
                ) * inv_ref[plane]
        return carry

    lax.fori_loop(0, loads, one_load, 0)


def smoother(sides, loads, modulus, halos):
    channels, planes, rows, cols = loads.shape
    vmem = pltpu.MemorySpace.VMEM
    return pl.pallas_call(
        smoother_kernel,
        out_shape=jax.ShapeDtypeStruct(loads.shape, jnp.float32),
        in_specs=[pl.BlockSpec(memory_space=pltpu.MemorySpace.SMEM)]
        + [pl.BlockSpec(memory_space=vmem)] * (2 + len(halos)),
        out_specs=pl.BlockSpec(memory_space=vmem),
        scratch_shapes=[
            pltpu.VMEM((2, len(OFFSETS), planes, rows, cols), jnp.float32),
            pltpu.VMEM((6, planes, rows, cols), jnp.float32),
            pltpu.VMEM((planes, rows, cols), jnp.float32),
            pltpu.VMEM((2, channels + 1, planes, cols), jnp.float32),
            pltpu.VMEM((2, channels + 1, planes, 2 * rows, cols), jnp.float32),
        ],
    )(sides, loads, modulus, *halos)


def per_device_body(right_sides, modulus, margin_sides, coarse_vectors, coarse_inverse):
    load_count = right_sides.shape[0]
    plane_count = right_sides.shape[2]
    row_count = right_sides.shape[3]
    column_count = right_sides.shape[4]
    cell_dims = (1, 2, 3, 4)
    partial_terms = lax.dot_general(
        coarse_vectors, right_sides, ((cell_dims, cell_dims), ((), ())), precision=lax.Precision.HIGHEST
    )

    loads = right_sides.reshape(load_count * 3, plane_count, row_count, column_count)
    row_first, row_last, col_first, col_last = pack(loads, modulus, partial_terms)
    rows_n = lax.axis_size("prow")
    cols_n = lax.axis_size("pcol")

    def line(source, axis, size, step):
        pairs = [(i, i + step) for i in range(size) if 0 <= i + step < size]
        return lax.ppermute(source, axis, pairs)

    row_lo = line(row_last, "prow", rows_n, 1)
    row_hi = line(row_first, "prow", rows_n, -1)
    vectors, terms = partial_terms.shape
    even = lax.axis_index("prow") % 2 == 0
    partner = jnp.where(even, row_hi[-vectors:, :terms], row_lo[-vectors:, :terms])
    ext_first, ext_last = edges(row_lo, row_hi, col_first, col_last)
    halos = (row_lo, row_hi, line(ext_last, "pcol", cols_n, 1), line(ext_first, "pcol", cols_n, -1))
    sides = margin_sides[0, 0].astype(jnp.float32)

    def smooth():
        return smoother(sides, loads, modulus, halos)

    restricted, smoothed = butterfly_sum(partial_terms + partner, "prow", 2, smooth)

    solved = jnp.dot(coarse_inverse[0], restricted, precision=lax.Precision.HIGHEST)
    lifted = lax.dot_general(
        solved, coarse_vectors, (((0,), (0,)), ((), ())), precision=lax.Precision.HIGHEST
    )
    return smoothed.reshape(right_sides.shape) + lifted


def solution(mesh):
    in_specs = (
        P(None, None, None, "prow", "pcol"),
        P(None, "prow", "pcol"),
        P("prow", "pcol", None),
        P(None, None, None, "prow", "pcol"),
        P("pcol", None, None),
    )
    out_specs = P(None, None, None, "prow", "pcol")
    return jax.shard_map(
        per_device_body, mesh=mesh, in_specs=in_specs, out_specs=out_specs, check_vma=False
    )
```

```python
import jax
import jax.numpy as jnp
from jax import lax
from jax.experimental import pallas as pl
from jax.experimental.pallas import tpu as pltpu
from jax.sharding import PartitionSpec as P


RELAX_WEIGHT = 0.7
MASS_SHIFT = 0.5
DIAGONAL_SLOPE = 0.6 + 0.4 / 3.0
BOND_TOTAL = 44.0 / 3.0

OFFSETS = [
    (step_p, step_x, step_y)
    for step_p in (-1, 0, 1)
    for step_x in (-1, 0, 1)
    for step_y in (-1, 0, 1)
    if (step_p, step_x, step_y) != (0, 0, 0)
]
OWN_ENTRIES = ((0, 0), (1, 1), (2, 2), (0, 1), (0, 2), (1, 2))


def butterfly_sum(x, axis, step=1):
    size = lax.axis_size(axis)
    if step < size:
        x = x + lax.ppermute(x, axis, [(i, i ^ step) for i in range(size)])
        step *= 2
    masks = [0]
    while step < size:
        masks = masks + [m | step for m in masks]
        step *= 2
    received = [lax.ppermute(x, axis, [(i, i ^ m) for i in range(size)]) for m in masks[1:]]
    for part in received:
        x = x + part
    return x


def neighbour_shift(tile, row_lo, row_hi, col_lo, col_hi, step_x, step_y):
    rows, cols = tile.shape
    if step_x != 0:
        rolled = pltpu.roll(tile, (-step_x) % rows, 0)
        sub = lax.broadcasted_iota(jnp.int32, tile.shape, 0)
        edge = rows - 1 if step_x > 0 else 0
        halo = row_hi if step_x > 0 else row_lo
        tile = jnp.where(sub == edge, jnp.broadcast_to(halo, tile.shape), rolled)
    if step_y != 0:
        rolled = pltpu.roll(tile, (-step_y) % cols, 1)
        lane = lax.broadcasted_iota(jnp.int32, tile.shape, 1)
        edge = cols - 1 if step_y > 0 else 0
        halo = col_hi if step_y > 0 else col_lo
        tile = jnp.where(lane == edge, jnp.broadcast_to(halo, tile.shape), rolled)
    return tile


def pack_kernel(rs_ref, mod_ref, partial_ref, row_first_ref, row_last_ref, col_first_ref, col_last_ref):
    channels, planes, rows, cols = rs_ref.shape
    count = (channels + 1) * planes
    lane = lax.broadcasted_iota(jnp.int32, (rows, cols), 1)
    tiles = col_first_ref.shape[1] // cols
    pad_from = count // rows * rows
    padding = jnp.zeros((row_first_ref.shape[0] - pad_from, cols), jnp.float32)
    row_first_ref[pl.ds(pad_from, padding.shape[0]), :] = padding
    row_last_ref[pl.ds(pad_from, padding.shape[0]), :] = padding
    first = [jnp.zeros((rows, cols), jnp.float32) for _ in range(tiles)]
    last = [jnp.zeros((rows, cols), jnp.float32) for _ in range(tiles)]
    for channel in range(channels + 1):
        for plane in range(planes):
            tile = rs_ref[channel, plane] if channel < channels else mod_ref[plane]
            j = channel * planes + plane
            row_first_ref[pl.ds(j, 1), :] = tile[0:1, :]
            row_last_ref[pl.ds(j, 1), :] = tile[rows - 1 : rows, :]
            group, place = divmod(j, cols)
            first[group] = jnp.where(lane == place, pltpu.roll(tile, place, 1), first[group])
            last[group] = jnp.where(
                lane == place, pltpu.roll(tile, (place + 1) % cols, 1), last[group]
            )
    for group in range(tiles):
        col_first_ref[:, pl.ds(group * cols, cols)] = first[group]
        col_last_ref[:, pl.ds(group * cols, cols)] = last[group]
    vectors, terms = partial_ref.shape
    start = row_first_ref.shape[0] - vectors
    row_first_ref[pl.ds(start, vectors), pl.ds(0, terms)] = partial_ref[...]
    row_last_ref[pl.ds(start, vectors), pl.ds(0, terms)] = partial_ref[...]


def pack(loads, modulus, partial):
    channels, planes, rows, cols = loads.shape
    count = (channels + 1) * planes
    lanes = -(-count // cols) * cols
    height = -(-(count + partial.shape[0]) // cols) * cols
    vmem = pltpu.MemorySpace.VMEM
    return pl.pallas_call(
        pack_kernel,
        out_shape=[
            jax.ShapeDtypeStruct((height, cols), jnp.float32),
            jax.ShapeDtypeStruct((height, cols), jnp.float32),
            jax.ShapeDtypeStruct((rows, lanes), jnp.float32),
            jax.ShapeDtypeStruct((rows, lanes), jnp.float32),
        ],
        in_specs=[pl.BlockSpec(memory_space=vmem)] * 3,
        out_specs=[pl.BlockSpec(memory_space=vmem)] * 4,
    )(loads, modulus, partial)


def edge_kernel(rlo_ref, rhi_ref, col_first_ref, col_last_ref, ext_first_ref, ext_last_ref):
    rows, lanes = col_first_ref.shape
    cols = rlo_ref.shape[1]
    low = jnp.transpose(rlo_ref[...])[:, 0:lanes]
    high = jnp.transpose(rhi_ref[...])[:, 0:lanes]
    zeros = jnp.zeros((ext_first_ref.shape[0] - rows - 2, lanes), jnp.float32)
    for out_ref, column, lane in ((ext_first_ref, col_first_ref, 0), (ext_last_ref, col_last_ref, cols - 1)):
        out_ref[pl.ds(0, 1), :] = low[lane : lane + 1, :]
        out_ref[pl.ds(1, rows), :] = column[...]
        out_ref[pl.ds(rows + 1, 1), :] = high[lane : lane + 1, :]
        out_ref[pl.ds(rows + 2, zeros.shape[0]), :] = zeros


def edges(row_lo, row_hi, col_first, col_last):
    rows, lanes = col_first.shape
    vmem = pltpu.MemorySpace.VMEM
    return pl.pallas_call(
        edge_kernel,
        out_shape=[jax.ShapeDtypeStruct((2 * rows, lanes), jnp.float32)] * 2,
        in_specs=[pl.BlockSpec(memory_space=vmem)] * 4,
        out_specs=[pl.BlockSpec(memory_space=vmem)] * 2,
    )(row_lo, row_hi, col_first, col_last)


def smoother_kernel(
    sides_ref, rs_ref, mod_ref, rlo_ref, rhi_ref, clo_ref, chi_ref,
    out_ref, coef_ref, own_ref, inv_ref, row_ref, col_ref,
):
    channels, planes, rows, cols = rs_ref.shape
    loads = channels // 3
    mod_channel = channels
    shape = (rows, cols)
    sub = lax.broadcasted_iota(jnp.int32, shape, 0)
    lane = lax.broadcasted_iota(jnp.int32, shape, 1)
    one = jnp.ones(shape, jnp.float32)
    factor_x = {
        -1: jnp.where(sub == 0, sides_ref[0], one),
        0: None,
        1: jnp.where(sub == rows - 1, sides_ref[1], one),
    }
    factor_y = {
        -1: jnp.where(lane == 0, sides_ref[2], one),
        0: None,
        1: jnp.where(lane == cols - 1, sides_ref[3], one),
    }

    def halo_pieces(channel, plane, step_x):
        row_lo = row_ref[0, channel, pl.ds(plane, 1), :]
        row_hi = row_ref[1, channel, pl.ds(plane, 1), :]
        col_lo = col_ref[0, channel, plane, pl.ds(1 + step_x, rows), :]
        col_hi = col_ref[1, channel, plane, pl.ds(1 + step_x, rows), :]
        return row_lo, row_hi, col_lo, col_hi

    for channel in range(channels + 1):
        row_ref[0, channel] = rlo_ref[pl.ds(channel * planes, planes), :]
        row_ref[1, channel] = rhi_ref[pl.ds(channel * planes, planes), :]
        for plane in range(planes):
            j = channel * planes + plane
            group, place = divmod(j, cols)
            window = pl.ds(group * cols, cols)
            for side, (edge, column) in enumerate(((0, clo_ref), (cols - 1, chi_ref))):
                col_ref[side, channel, plane] = pltpu.roll(
                    column[:, window], (edge - place) % cols, 1
                )
    row_inverse = RELAX_WEIGHT / (MASS_SHIFT + DIAGONAL_SLOPE * row_ref[:, mod_channel : mod_channel + 1])
    row_ref[:, 0:channels] = row_ref[:, 0:channels] * row_inverse
    col_inverse = RELAX_WEIGHT / (MASS_SHIFT + DIAGONAL_SLOPE * col_ref[:, mod_channel : mod_channel + 1, :, 0 : rows + 2])
    col_ref[:, 0:channels, :, 0 : rows + 2] = col_ref[:, 0:channels, :, 0 : rows + 2] * col_inverse

    for plane in range(planes):
        own_modulus = mod_ref[plane]
        inv_ref[plane] = 1.0 / (MASS_SHIFT + DIAGONAL_SLOPE * own_modulus)
        own = [None] * 6
        for index, (step_p, step_x, step_y) in enumerate(OFFSETS):
            source = plane + step_p
            length = step_p * step_p + step_x * step_x + step_y * step_y
            weight = 1.0 / (length * BOND_TOTAL)
            if 0 <= source < planes:
                pieces = halo_pieces(mod_channel, source, step_x)
                near_modulus = neighbour_shift(mod_ref[source], *pieces, step_x, step_y)
                bond = (0.5 * weight) * (own_modulus + near_modulus)
                coefficient = bond
                if factor_x[step_x] is not None:
                    coefficient = coefficient * factor_x[step_x]
                if factor_y[step_y] is not None:
                    coefficient = coefficient * factor_y[step_y]
                coef_ref[0, index, plane] = 0.6 * coefficient
                coef_ref[1, index, plane] = (0.4 / length) * coefficient
            else:
                bond = (0.5 * weight) * own_modulus
            direction = (step_p, step_x, step_y)
            for entry, (a, b) in enumerate(OWN_ENTRIES):
                scale = 0.4 * direction[a] * direction[b] / length
                if a == b:
                    scale += 0.6
                if scale == 0.0:
                    continue
                term = scale * bond
                own[entry] = term if own[entry] is None else own[entry] + term
        for entry, (a, b) in enumerate(OWN_ENTRIES):
            value = own[entry]
            if a == b:
                value = value + MASS_SHIFT
            own_ref[entry, plane] = value

    def one_load(load, carry):
        base = load * 3
        first = [[None] * planes for _ in range(3)]
        for component in range(3):
            for plane in range(planes):
                first[component][plane] = (
                    RELAX_WEIGHT * rs_ref[base + component, plane] * inv_ref[plane]
                )
        applied = [[None] * 3 for _ in range(planes)]
        for plane in range(planes):
            f = [first[k][plane] for k in range(3)]
            own = [own_ref[e, plane] for e in range(6)]
            applied[plane][0] = own[0] * f[0] + own[3] * f[1] + own[4] * f[2]
            applied[plane][1] = own[3] * f[0] + own[1] * f[1] + own[5] * f[2]
            applied[plane][2] = own[4] * f[0] + own[5] * f[1] + own[2] * f[2]
        for source in range(planes):
            for step_x in (-1, 0, 1):
                for step_y in (-1, 0, 1):
                    targets = [
                        (source - step_p, step_p)
                        for step_p in (-1, 0, 1)
                        if 0 <= source - step_p < planes and (step_p, step_x, step_y) != (0, 0, 0)
                    ]
                    if not targets:
                        continue
                    near = []
                    for component in range(3):
                        pieces = halo_pieces(base + component, source, step_x)
                        near.append(
                            neighbour_shift(first[component][source], *pieces, step_x, step_y)
                        )
                    for plane, step_p in targets:
                        direction = (step_p, step_x, step_y)
                        index = OFFSETS.index(direction)
                        projected = None
                        for component in range(3):
                            if direction[component] == 0:
                                continue
                            term = near[component]
                            if projected is None:
                                projected = term if direction[component] > 0 else -term
                            elif direction[component] > 0:
                                projected = projected + term
                            else:
                                projected = projected - term
                        along = coef_ref[1, index, plane] * projected
                        straight = coef_ref[0, index, plane]
                        for component in range(3):
                            value = applied[plane][component] - straight * near[component]
                            if direction[component] > 0:
                                value = value - along
                            elif direction[component] < 0:
                                value = value + along
                            applied[plane][component] = value
        for component in range(3):
            for plane in range(planes):
                load_tile = rs_ref[base + component, plane]
                out_ref[base + component, plane] = first[component][plane] + RELAX_WEIGHT * (
                    load_tile - applied[plane][component]
                ) * inv_ref[plane]
        return carry

    lax.fori_loop(0, loads, one_load, 0)


def smoother(sides, loads, modulus, halos):
    channels, planes, rows, cols = loads.shape
    vmem = pltpu.MemorySpace.VMEM
    return pl.pallas_call(
        smoother_kernel,
        out_shape=jax.ShapeDtypeStruct(loads.shape, jnp.float32),
        in_specs=[pl.BlockSpec(memory_space=pltpu.MemorySpace.SMEM)]
        + [pl.BlockSpec(memory_space=vmem)] * (2 + len(halos)),
        out_specs=pl.BlockSpec(memory_space=vmem),
        scratch_shapes=[
            pltpu.VMEM((2, len(OFFSETS), planes, rows, cols), jnp.float32),
            pltpu.VMEM((6, planes, rows, cols), jnp.float32),
            pltpu.VMEM((planes, rows, cols), jnp.float32),
            pltpu.VMEM((2, channels + 1, planes, cols), jnp.float32),
            pltpu.VMEM((2, channels + 1, planes, 2 * rows, cols), jnp.float32),
        ],
    )(sides, loads, modulus, *halos)


def per_device_body(right_sides, modulus, margin_sides, coarse_vectors, coarse_inverse):
    load_count = right_sides.shape[0]
    plane_count = right_sides.shape[2]
    row_count = right_sides.shape[3]
    column_count = right_sides.shape[4]
    cell_dims = (1, 2, 3, 4)
    partial_terms = lax.dot_general(
        coarse_vectors, right_sides, ((cell_dims, cell_dims), ((), ())), precision=lax.Precision.HIGHEST
    )

    loads = right_sides.reshape(load_count * 3, plane_count, row_count, column_count)
    row_first, row_last, col_first, col_last = pack(loads, modulus, partial_terms)
    rows_n = lax.axis_size("prow")
    cols_n = lax.axis_size("pcol")

    def line(source, axis, size, step):
        pairs = [(i, i + step) for i in range(size) if 0 <= i + step < size]
        return lax.ppermute(source, axis, pairs)

    row_lo = line(row_last, "prow", rows_n, 1)
    row_hi = line(row_first, "prow", rows_n, -1)
    vectors, terms = partial_terms.shape
    even = lax.axis_index("prow") % 2 == 0
    partner = jnp.where(even, row_hi[-vectors:, :terms], row_lo[-vectors:, :terms])
    ext_first, ext_last = edges(row_lo, row_hi, col_first, col_last)
    halos = (row_lo, row_hi, line(ext_last, "pcol", cols_n, 1), line(ext_first, "pcol", cols_n, -1))
    sides = margin_sides[0, 0].astype(jnp.float32)

    smoothed = smoother(sides, loads, modulus, halos)
    restricted = butterfly_sum(partial_terms + partner, "prow", 2)

    solved = jnp.dot(coarse_inverse[0], restricted, precision=lax.Precision.HIGHEST)
    lifted = lax.dot_general(
        solved, coarse_vectors, (((0,), (0,)), ((), ())), precision=lax.Precision.HIGHEST
    )
    return smoothed.reshape(right_sides.shape) + lifted


def solution(mesh):
    in_specs = (
        P(None, None, None, "prow", "pcol"),
        P(None, "prow", "pcol"),
        P("prow", "pcol", None),
        P(None, None, None, "prow", "pcol"),
        P("pcol", None, None),
    )
    out_specs = P(None, None, None, "prow", "pcol")
    return jax.shard_map(
        per_device_body, mesh=mesh, in_specs=in_specs, out_specs=out_specs, check_vma=False
    )
```
